512 devices in a mesh: space: 64 (over x, y, core), chan: 8 (over z).
Axes of the slice: x: 4, y: 8, z: 8, core: 2. Of those that a mesh axis runs over, the one named last changes fastest.
Arguments:
- features: bfloat16 [128, 64, 4096], P('space', 'chan'), may hold values from -6 to 6
- conv_weight: bfloat16 [128, 9, 64], P('chan'), may hold values from -0.25 to 0.25
- down_weight: bfloat16 [128, 4, 128], P('chan'), may hold values from -0.25 to 0.25
- cotangent: bfloat16 [128, 128, 1024], P('space', 'chan'), may hold values from -16 to 16
- partner: int32 [128, 4], P('space'), may hold values from 0 to 511, as said below
- orientation: int32 [128, 4], P('space'), may hold values from 0 to 1, as said below
Outputs:
- pooled: bfloat16 [128, 128, 1024], P('space', 'chan')
- features_grad: bfloat16 [128, 64, 4096], P('space', 'chan')
- conv_grad: float32 [128, 9, 64], P('chan')
- down_grad: float32 [128, 4, 128], P('chan')
The draws below stay inside these ranges and needn't reach their ends.
Inputs may be any that keep to these rules, and one draw needn't show every extreme that they name: Bordering is mutual: the slot at partner[t, e] has partner 4 t + e; no edge borders itself; every slot 0 to 511 appears exactly once. `orientation`: both edges of a bordering pair carry the same value.
All inputs are finite; a program needn't handle non-finite values.
Results may differ from the reference program's by a relative error of at most 0.0049.
Values may be sent and summed in bfloat16 or wider, within the bound.
No kernel may reach another device: no remote copies, remote signals or barrier semaphores. Data moves between devices by JAX's collectives and lax.ppermute only.
A program may use at most 64 MiB of HBM per device.

```python
import jax
import jax.numpy as jnp
from jax import lax

CIN = 64
COUT = 128
S = 64
TILES = 128


def matching(key):
    slots = 4 * TILES
    order = jax.random.permutation(jax.random.fold_in(key, 11), slots).astype(jnp.int32)
    first = order[0::2]
    second = order[1::2]
    partner = jnp.zeros((slots,), jnp.int32).at[first].set(second).at[second].set(first)
    choices_bits = jax.random.randint(jax.random.fold_in(key, 12), (slots // 2,), 0, 2).astype(jnp.int32)
    choices_bits = choices_bits.at[0].set(1).at[1].set(0)
    flags = jnp.zeros((slots,), jnp.int32).at[first].set(choices_bits).at[second].set(choices_bits)
    return (partner.reshape(TILES, 4), flags.reshape(TILES, 4))


def draw_partner(key, part):
    return matching(key)[0]


def draw_orientation(key, part):
    return matching(key)[1]


def spiked(values, own_key, source, target, shards_of, factor):
    def block_of(axis_at):
        return (jnp.arange(values.shape[axis_at]) // (values.shape[axis_at] // shards_of)).reshape((-1,) + (1,) * (values.ndim - 1 - axis_at))

    one_side = jax.random.permutation(own_key, shards_of)[block_of(target)]
    far = (block_of(target) + shards_of // 2) % shards_of
    return jnp.where((block_of(source) == one_side) | (block_of(source) == far), factor * values, values)


def steps_of(stream_key, shape, split, smallest, largest):
    factor_of, own = 1.0, jax.random.fold_in(stream_key, 6)
    for axis_at, shards_of in split:
        steps = jnp.exp(jax.random.uniform(jax.random.fold_in(own, axis_at), (shards_of,), jnp.float32, smallest / len(split), largest / len(split)))
        factor_of = factor_of * jnp.repeat(steps, shape[axis_at] // shards_of).reshape([-1 if axis == axis_at else 1 for axis in range(len(shape))])
    return factor_of


def gaussian(key, extent, deviation, most, shards=(), dtype=jnp.bfloat16):
    array = deviation * jax.random.normal(key, extent, jnp.float32)
    if shards:
        array = array * steps_of(key, extent, shards, -0.22, 0.18)
    return jnp.clip(array, -most, most).astype(dtype)


def heavy_noise(key, dims, deviation, bound, shards, heavy, kind=jnp.bfloat16):
    values = deviation * jax.random.normal(key, dims, jnp.float32)
    if shards:
        values = values * steps_of(key, dims, shards, -0.22, 0.18)
    return jnp.clip(spiked(values, jax.random.fold_in(key, 3), *heavy), -bound, bound).astype(kind)


def setup_inputs(seed: int = 0) -> dict:
    keys = jax.random.split(jax.random.key(seed), 7)
    return {
        "features": gaussian(keys[0], (TILES, CIN, S * S), 1.0, 6.0, ((0, 64), (1, 8))),
        "conv_weight": gaussian(keys[1], (COUT, 9, CIN), (9 * CIN) ** -0.5, 0.25, ((0, 8),)),
        "down_weight": gaussian(keys[2], (COUT, 4, COUT), (4 * COUT) ** -0.5, 0.25, ((0, 8),)),
        "cotangent": heavy_noise(keys[3], (TILES, COUT, (S // 2) * (S // 2)), 1.0, 16.0, ((0, 64), (1, 8)), (0, 1, 64, 4.0)),
        "partner": draw_partner(jax.random.fold_in(keys[6], 71), 0),
        "orientation": draw_orientation(jax.random.fold_in(keys[6], 71), 0),
    }


def edge_strips(values):
    return jnp.stack([values[..., 0, :], values[..., :, -1], values[..., -1, :], values[..., :, 0]], axis=-3)

def rim_strips(padded):
    return jnp.stack([padded[..., 0, 1:-1], padded[..., 1:-1, -1], padded[..., -1, 1:-1], padded[..., 1:-1, 0]], axis=-3)

def bordering(strips, partner, orientation):
    flat = strips.reshape((-1,) + strips.shape[2:])
    picked = jnp.take(flat, partner.reshape(-1).astype(jnp.int32), axis=0)
    picked = picked.reshape(partner.shape + strips.shape[2:])
    return jnp.where((orientation == 1)[..., None, None], picked[..., ::-1], picked)

def pad_tile(values, halo_strips):
    tile_side = values.shape[-1]
    widths = [(0, 0)] * (values.ndim - 2) + [(1, 1), (1, 1)]
    padded = jnp.pad(values, widths)
    padded = padded.at[..., 0, 1:tile_side + 1].set(halo_strips[..., 0, :, :])
    padded = padded.at[..., 1:tile_side + 1, tile_side + 1].set(halo_strips[..., 1, :, :])
    padded = padded.at[..., tile_side + 1, 1:tile_side + 1].set(halo_strips[..., 2, :, :])
    return padded.at[..., 1:tile_side + 1, 0].set(halo_strips[..., 3, :, :])

def add_edges(interior, returned):
    interior = interior.at[..., 0, :].add(returned[..., 0, :, :])
    interior = interior.at[..., :, -1].add(returned[..., 1, :, :])
    interior = interior.at[..., -1, :].add(returned[..., 2, :, :])
    return interior.at[..., :, 0].add(returned[..., 3, :, :])

def unfold(padded, height, width):
    taps = [padded[..., row_shift:row_shift + height, col_shift:col_shift + width] for row_shift in range(3) for col_shift in range(3)]
    return jnp.stack(taps, axis=-4)

def fold_taps(taps):
    total = None
    for row_shift in range(3):
        for col_shift in range(3):
            piece = taps[..., 3 * row_shift + col_shift, :, :, :]
            widths = [(0, 0)] * (piece.ndim - 2) + [(row_shift, 2 - row_shift), (col_shift, 2 - col_shift)]
            placed = jnp.pad(piece, widths)
            total = placed if total is None else total + placed
    return total

def silu_grad(values):
    gate = jax.nn.sigmoid(values)
    return gate * (1.0 + values * (1.0 - gate))

def tile_pass(conv_weight, down_weight, tile_in, halo_tile, grad_tile):
    tile_side = tile_in.shape[-1]
    out_channels = conv_weight.shape[0]
    padded = pad_tile(tile_in, halo_tile)
    columns = unfold(padded, tile_side, tile_side).astype(jnp.float32)
    conv_wide = conv_weight.astype(jnp.float32)
    pre_act = jnp.einsum('okc,kcrs->ors', conv_wide, columns)
    activated = jax.nn.silu(pre_act).astype(jnp.bfloat16)
    quads = activated.reshape(out_channels, tile_side // 2, 2, tile_side // 2, 2).astype(jnp.float32)
    down_taps = down_weight.reshape(out_channels, 2, 2, out_channels).astype(jnp.float32)
    grad_wide = grad_tile.astype(jnp.float32)
    pooled = jnp.einsum('opqc,cipjq->oij', down_taps, quads).astype(jnp.bfloat16)
    down_part = jnp.einsum('oij,cipjq->opqc', grad_wide, quads).reshape(out_channels, 4, out_channels)
    grad_act = jnp.einsum('opqc,oij->cipjq', down_taps, grad_wide).reshape(out_channels, tile_side, tile_side)
    grad_pre = (grad_act * silu_grad(pre_act)).astype(jnp.bfloat16).astype(jnp.float32)
    conv_part = jnp.einsum('ors,kcrs->okc', grad_pre, columns)
    grad_padded = fold_taps(jnp.einsum('okc,ors->kcrs', conv_wide, grad_pre))
    return (pooled, conv_part, down_part, grad_padded)

def reference(features, conv_weight, down_weight, cotangent, partner, orientation):
    tile_count = features.shape[0]
    out_channels = conv_weight.shape[0]
    in_channels = conv_weight.shape[2]
    images = features.reshape(tile_count, in_channels, S, S)
    grad_images = cotangent.reshape(tile_count, out_channels, S // 2, S // 2)
    halo_all = bordering(edge_strips(images), partner, orientation)

    def one_tile(totals, inputs_tile):
        tile_in, halo_tile, grad_tile = inputs_tile
        pooled, conv_part, down_part, grad_padded = tile_pass(conv_weight, down_weight, tile_in, halo_tile, grad_tile)
        new_totals = (totals[0] + conv_part, totals[1] + down_part)
        return (new_totals, (pooled, grad_padded[:, 1:-1, 1:-1], rim_strips(grad_padded)))
    start = (jnp.zeros((out_channels, 9, in_channels), jnp.float32), jnp.zeros((out_channels, 4, out_channels), jnp.float32))
    totals, outputs = lax.scan(one_tile, start, (images, halo_all, grad_images))
    pooled, interior, rims = outputs
    returned = bordering(rims, partner, orientation)
    features_grad = add_edges(interior, returned).astype(jnp.bfloat16)
    grad_scale = float(TILES * S * S) ** (-0.5)
    pooled_flat = pooled.reshape(tile_count, out_channels, S // 2 * (S // 2))
    grad_flat = features_grad.reshape(tile_count, in_channels, S * S)
    return (pooled_flat, grad_flat, totals[0] * grad_scale, totals[1] * grad_scale)
```

```python
import jax
import jax.numpy as jnp
from jax import lax
from jax.sharding import PartitionSpec as P

S = 64
F32 = jnp.float32
BF16 = jnp.bfloat16


def edge_strips(values):
    return jnp.stack(
        [values[..., 0, :], values[..., :, -1], values[..., -1, :], values[..., :, 0]], axis=-3
    )


def rim_strips(padded):
    return jnp.stack(
        [padded[..., 0, 1:-1], padded[..., 1:-1, -1], padded[..., -1, 1:-1], padded[..., 1:-1, 0]],
        axis=-3,
    )


def bordering(strips, partner, orientation):
    flat = strips.reshape((-1,) + strips.shape[2:])
    picked = jnp.take(flat, partner.reshape(-1), axis=0)
    picked = picked.reshape(partner.shape + strips.shape[2:])
    return jnp.where((orientation == 1)[..., None, None], picked[..., ::-1], picked)


def pad_tile(values, halo_strips):
    tile_side = values.shape[-1]
    widths = [(0, 0)] * (values.ndim - 2) + [(1, 1), (1, 1)]
    padded = jnp.pad(values, widths)
    padded = padded.at[..., 0, 1 : tile_side + 1].set(halo_strips[..., 0, :, :])
    padded = padded.at[..., 1 : tile_side + 1, tile_side + 1].set(halo_strips[..., 1, :, :])
    padded = padded.at[..., tile_side + 1, 1 : tile_side + 1].set(halo_strips[..., 2, :, :])
    return padded.at[..., 1 : tile_side + 1, 0].set(halo_strips[..., 3, :, :])


def add_edges(interior, returned):
    interior = interior.at[..., 0, :].add(returned[..., 0, :, :])
    interior = interior.at[..., :, -1].add(returned[..., 1, :, :])
    interior = interior.at[..., -1, :].add(returned[..., 2, :, :])
    return interior.at[..., :, 0].add(returned[..., 3, :, :])


def unfold(padded, height, width):
    taps = [
        padded[..., row_shift : row_shift + height, col_shift : col_shift + width]
        for row_shift in range(3)
        for col_shift in range(3)
    ]
    return jnp.stack(taps, axis=-4)


def fold_taps(taps):
    total = None
    for row_shift in range(3):
        for col_shift in range(3):
            piece = taps[..., 3 * row_shift + col_shift, :, :, :]
            widths = [(0, 0)] * (piece.ndim - 2) + [
                (row_shift, 2 - row_shift),
                (col_shift, 2 - col_shift),
            ]
            placed = jnp.pad(piece, widths)
            total = placed if total is None else total + placed
    return total


def silu_grad(values):
    gate = jax.nn.sigmoid(values)
    return gate * (1.0 + values * (1.0 - gate))


def exchange(parts, axis):
    count = parts[0].shape[0]
    flat = [p.reshape(count, -1) for p in parts]
    sizes = [f.shape[1] for f in flat]
    got = lax.all_to_all(jnp.concatenate(flat, axis=1), axis, 0, 0, tiled=True)
    out, start = [], 0
    for p, size in zip(parts, sizes):
        out.append(got[:, start : start + size].reshape(p.shape))
        start += size
    return out


def to_all(value, count):
    return jnp.broadcast_to(value[None], (count,) + value.shape)


def split_wide(value):
    high = lax.reduce_precision(value, exponent_bits=8, mantissa_bits=7)
    return jnp.stack([high, value - high], axis=1).astype(BF16)


def shards(features, conv_weight, down_weight, cotangent, partner, orientation):
    tiles, share, _ = features.shape
    n_chan = lax.axis_size("chan")
    n_space = lax.axis_size("space")
    in_channels = share * n_chan
    out_share = conv_weight.shape[0]
    out_channels = out_share * n_chan
    rows = S // n_chan
    half = S // 2
    conv_cols = conv_weight.shape[1] * conv_weight.shape[2]
    down_cols = down_weight.shape[1] * down_weight.shape[2]

    images = features.reshape(tiles, share, S, S)
    strips = edge_strips(images)
    (strips_all,) = exchange([to_all(strips, n_space)], "space")
    halo = bordering(strips_all.reshape((n_space * tiles,) + strips.shape[1:]), partner, orientation)
    padded = pad_tile(images, halo)

    bands = jnp.stack([padded[:, :, rows * b : rows * b + rows + 2, :] for b in range(n_chan)])
    cot_bands = jnp.moveaxis(cotangent.reshape(tiles, out_share, n_chan, rows // 2 * half), 2, 0)
    weights = jnp.concatenate(
        [conv_weight.reshape(out_share, conv_cols), down_weight.reshape(out_share, down_cols)], axis=1
    )
    band_in, cot_in, w_in = exchange([bands, cot_bands, to_all(weights, n_chan)], "chan")
    block = jnp.moveaxis(band_in, 0, 1).reshape(tiles, in_channels, rows + 2, S + 2)
    grad_band = jnp.moveaxis(cot_in, 0, 1).reshape(tiles, out_channels, rows // 2, half)
    w_full = w_in.reshape(out_channels, conv_cols + down_cols)
    conv_full = w_full[:, :conv_cols].reshape(out_channels, 9, in_channels)
    down_full = w_full[:, conv_cols:].reshape(out_channels, 4, out_channels)

    columns = unfold(block, rows, S)
    pre_act = jnp.einsum("okc,tkcrs->tors", conv_full, columns, preferred_element_type=F32)
    activated = jax.nn.silu(pre_act).astype(BF16)
    quads = activated.reshape(tiles, out_channels, rows // 2, 2, half, 2)
    down_taps = down_full.reshape(out_channels, 2, 2, out_channels)
    pooled_rows = jnp.einsum(
        "opqc,tcipjq->toij", down_taps, quads, preferred_element_type=F32
    ).astype(BF16)
    down_part = jnp.einsum("toij,tcipjq->opqc", grad_band, quads, preferred_element_type=F32)
    down_part = down_part.reshape(out_channels, down_cols)
    grad_act = jnp.einsum("opqc,toij->tcipjq", down_taps, grad_band, preferred_element_type=F32)
    grad_act = grad_act.reshape(tiles, out_channels, rows, S)
    grad_pre = (grad_act * silu_grad(pre_act)).astype(BF16)
    conv_part = jnp.einsum("tors,tkcrs->okc", grad_pre, columns, preferred_element_type=F32)
    grad_block = fold_taps(
        jnp.einsum("okc,tors->tkcrs", conv_full, grad_pre, preferred_element_type=F32)
    )

    pooled_out = jnp.moveaxis(pooled_rows.reshape(tiles, n_chan, out_share, rows // 2 * half), 1, 0)
    grad_out = jnp.moveaxis(
        grad_block.astype(BF16).reshape(tiles, n_chan, share, rows + 2, S + 2), 1, 0
    )
    w_part = jnp.concatenate([conv_part.reshape(out_channels, conv_cols), down_part], axis=1)
    w_part = split_wide(w_part.reshape(n_chan, out_share * (conv_cols + down_cols)))
    pooled_in, grad_in, w_back = exchange([pooled_out, grad_out, w_part], "chan")
    pooled = jnp.moveaxis(pooled_in, 0, 2).reshape(tiles, out_share, half * half)
    w_sum = jnp.sum(w_back.astype(F32), axis=(0, 1))

    g = grad_in.astype(F32)
    main = jnp.moveaxis(g[:, :, :, :rows, :], 0, 2).reshape(tiles, share, S, S + 2)
    extra = jnp.pad(g[:, :, :, rows:, :], ((0, 0), (0, 0), (0, 0), (0, rows - 2), (0, 0)))
    extra = jnp.moveaxis(extra, 0, 2).reshape(tiles, share, S, S + 2)
    grad_padded = jnp.pad(main, ((0, 0), (0, 0), (0, 2), (0, 0))) + jnp.pad(
        extra, ((0, 0), (0, 0), (rows, 0), (0, 0))
    )[:, :, : S + 2, :]

    rims = rim_strips(grad_padded)
    w_len = w_sum.shape[0]
    piece = -(-w_len // n_space)
    w_pieces = jnp.pad(w_sum, (0, piece * n_space - w_len)).reshape(n_space, piece)
    rims_all, w_got = exchange([to_all(rims, n_space), w_pieces], "space")
    w_mine = jnp.sum(w_got, axis=0)
    (w_all,) = exchange([to_all(w_mine, n_space)], "space")
    w_total = w_all.reshape(-1)[:w_len].reshape(out_share, conv_cols + down_cols)

    returned = bordering(rims_all.reshape((n_space * tiles,) + rims.shape[1:]), partner, orientation)
    features_grad = add_edges(grad_padded[:, :, 1:-1, 1:-1], returned).astype(BF16)
    features_grad = features_grad.reshape(tiles, share, S * S)
    grad_scale = float(n_space * tiles * S * S) ** (-0.5)
    conv_grad = w_total[:, :conv_cols].reshape(conv_weight.shape) * grad_scale
    down_grad = w_total[:, conv_cols:].reshape(down_weight.shape) * grad_scale
    return (pooled, features_grad, conv_grad, down_grad)


def solution(mesh):
    placed = (
        P("space", "chan", None),
        P("chan", None, None),
        P("chan", None, None),
        P("space", "chan", None),
        P("space", None),
        P("space", None),
    )
    return jax.shard_map(
        shards,
        mesh=mesh,
        in_specs=placed,
        out_specs=(
            P("space", "chan", None),
            P("space", "chan", None),
            P("chan", None, None),
            P("chan", None, None),
        ),
        check_vma=False,
    )
```

```python
import jax
import jax.numpy as jnp
from jax import lax
from jax.sharding import PartitionSpec as P

S = 64
F32 = jnp.float32
BF16 = jnp.bfloat16


def edge_strips(values):
    return jnp.stack(
        [values[..., 0, :], values[..., :, -1], values[..., -1, :], values[..., :, 0]], axis=-3
    )


def rim_strips(padded):
    return jnp.stack(
        [padded[..., 0, 1:-1], padded[..., 1:-1, -1], padded[..., -1, 1:-1], padded[..., 1:-1, 0]],
        axis=-3,
    )


def bordering(strips, partner, orientation):
    flat = strips.reshape((-1,) + strips.shape[2:])
    picked = jnp.take(flat, partner.reshape(-1), axis=0)
    picked = picked.reshape(partner.shape + strips.shape[2:])
    return jnp.where((orientation == 1)[..., None, None], picked[..., ::-1], picked)


def pad_tile(values, halo_strips):
    tile_side = values.shape[-1]
    widths = [(0, 0)] * (values.ndim - 2) + [(1, 1), (1, 1)]
    padded = jnp.pad(values, widths)
    padded = padded.at[..., 0, 1 : tile_side + 1].set(halo_strips[..., 0, :, :])
    padded = padded.at[..., 1 : tile_side + 1, tile_side + 1].set(halo_strips[..., 1, :, :])
    padded = padded.at[..., tile_side + 1, 1 : tile_side + 1].set(halo_strips[..., 2, :, :])
    return padded.at[..., 1 : tile_side + 1, 0].set(halo_strips[..., 3, :, :])


def pad_cat(values, halo):
    zero = jnp.zeros(values.shape[:2] + (1, 1), values.dtype)
    top = jnp.concatenate([zero, halo[:, 0, :, None, :], zero], axis=3)
    bottom = jnp.concatenate([zero, halo[:, 2, :, None, :], zero], axis=3)
    middle = jnp.concatenate([halo[:, 3, :, :, None], values, halo[:, 1, :, :, None]], axis=3)
    return jnp.concatenate([top, middle, bottom], axis=2)


def add_edges(interior, returned):
    n = interior.shape[-1]
    none = ((0, 0), (0, 0))
    rows = jnp.pad(returned[:, 0, :, None, :], none + ((0, n - 1), (0, 0))) + jnp.pad(
        returned[:, 2, :, None, :], none + ((n - 1, 0), (0, 0))
    )
    cols = jnp.pad(returned[:, 3, :, :, None], none + ((0, 0), (0, n - 1))) + jnp.pad(
        returned[:, 1, :, :, None], none + ((0, 0), (n - 1, 0))
    )
    return interior + (rows + cols)


def unfold(padded, height, width):
    taps = [
        padded[..., row_shift : row_shift + height, col_shift : col_shift + width]
        for row_shift in range(3)
        for col_shift in range(3)
    ]
    return jnp.stack(taps, axis=-4)


def fold_taps(taps):
    total = None
    for row_shift in range(3):
        for col_shift in range(3):
            piece = taps[..., 3 * row_shift + col_shift, :, :, :]
            widths = [(0, 0)] * (piece.ndim - 2) + [
                (row_shift, 2 - row_shift),
                (col_shift, 2 - col_shift),
            ]
            placed = jnp.pad(piece, widths)
            total = placed if total is None else total + placed
    return total


def silu_grad(values):
    gate = jax.nn.sigmoid(values)
    return gate * (1.0 + values * (1.0 - gate))


def exchange(parts, axis):
    count = parts[0].shape[0]
    flat = [p.reshape(count, -1) for p in parts]
    sizes = [f.shape[1] for f in flat]
    total = sum(sizes)
    lanes = -(-total // 128) * 128
    buf = jnp.concatenate(flat + [jnp.zeros((count, lanes - total), flat[0].dtype)], axis=1)
    got = lax.all_to_all(buf.reshape(count, lanes // 128, 128), axis, 0, 0, tiled=True)
    got = got.reshape(count, lanes)
    out, start = [], 0
    for p, size in zip(parts, sizes):
        out.append(got[:, start : start + size].reshape(p.shape))
        start += size
    return out


def to_all(value, count):
    return jnp.broadcast_to(value[None], (count,) + value.shape)


def split_wide(value):
    high = lax.reduce_precision(value, exponent_bits=8, mantissa_bits=7)
    return jnp.stack([high, value - high], axis=1).astype(BF16)


def shards(features, conv_weight, down_weight, cotangent, partner, orientation):
    tiles, share, _ = features.shape
    n_chan = lax.axis_size("chan")
    n_space = lax.axis_size("space")
    in_channels = share * n_chan
    out_share = conv_weight.shape[0]
    out_channels = out_share * n_chan
    rows = S // n_chan
    half = S // 2
    conv_cols = conv_weight.shape[1] * conv_weight.shape[2]
    down_cols = down_weight.shape[1] * down_weight.shape[2]

    images = features.reshape(tiles, share, S, S)
    strips = edge_strips(images)
    (strips_all,) = exchange([to_all(strips, n_space)], "space")
    halo = bordering(strips_all.reshape((n_space * tiles,) + strips.shape[1:]), partner, orientation)
    padded = pad_cat(images, halo)

    bands = jnp.stack([padded[:, :, rows * b : rows * b + rows + 2, :] for b in range(n_chan)])
    cot_bands = jnp.moveaxis(cotangent.reshape(tiles, out_share, n_chan, rows // 2 * half), 2, 0)
    weights = jnp.concatenate(
        [conv_weight.reshape(out_share, conv_cols), down_weight.reshape(out_share, down_cols)], axis=1
    )
    band_in, cot_in, w_in = exchange([bands, cot_bands, to_all(weights, n_chan)], "chan")
    block = jnp.moveaxis(band_in, 0, 1).reshape(tiles, in_channels, rows + 2, S + 2)
    grad_band = jnp.moveaxis(cot_in, 0, 1).reshape(tiles, out_channels, rows // 2, half)
    w_full = w_in.reshape(out_channels, conv_cols + down_cols)
    conv_full = w_full[:, :conv_cols].reshape(out_channels, 9, in_channels)
    down_full = w_full[:, conv_cols:].reshape(out_channels, 4, out_channels)

    plain = ("NCHW", "OIHW", "NCHW")
    swapped = ("CNHW", "IOHW", "NCHW")
    w_conv = conv_full.reshape(out_channels, 3, 3, in_channels).transpose(0, 3, 1, 2)
    w_down = down_full.reshape(out_channels, 2, 2, out_channels).transpose(0, 3, 1, 2)
    pre_act = lax.conv_general_dilated(
        block, w_conv, (1, 1), "VALID", dimension_numbers=plain, preferred_element_type=F32
    )
    activated = jax.nn.silu(pre_act).astype(BF16)
    pooled_rows = lax.conv_general_dilated(
        activated, w_down, (2, 2), "VALID", dimension_numbers=plain, preferred_element_type=F32
    ).astype(BF16)
    down_part = lax.conv_general_dilated(
        activated, grad_band, (1, 1), "VALID", rhs_dilation=(2, 2),
        dimension_numbers=swapped, preferred_element_type=F32,
    )
    down_part = down_part.transpose(1, 2, 3, 0).reshape(out_channels, down_cols)
    w_up = jnp.flip(w_down, (2, 3)).transpose(1, 0, 2, 3)
    grad_act = lax.conv_general_dilated(
        grad_band, w_up, (1, 1), ((1, 1), (1, 1)), lhs_dilation=(2, 2),
        dimension_numbers=plain, preferred_element_type=F32,
    )
    grad_pre = (grad_act * silu_grad(pre_act)).astype(BF16)
    conv_part = lax.conv_general_dilated(
        block, grad_pre, (1, 1), "VALID", dimension_numbers=swapped, preferred_element_type=F32
    )
    conv_part = conv_part.transpose(1, 2, 3, 0).reshape(out_channels, conv_cols)
    w_back_conv = jnp.flip(w_conv, (2, 3)).transpose(1, 0, 2, 3)
    grad_block = lax.conv_general_dilated(
        grad_pre, w_back_conv, (1, 1), ((2, 2), (2, 2)), dimension_numbers=plain,
        preferred_element_type=F32,
    )

    pooled_out = jnp.moveaxis(pooled_rows.reshape(tiles, n_chan, out_share, rows // 2 * half), 1, 0)
    grad_out = jnp.moveaxis(
        grad_block.astype(BF16).reshape(tiles, n_chan, share, rows + 2, S + 2), 1, 0
    )
    w_part = jnp.concatenate([conv_part, down_part], axis=1)
    w_part = split_wide(w_part.reshape(n_chan, out_share * (conv_cols + down_cols)))
    pooled_in, grad_in, w_back = exchange([pooled_out, grad_out, w_part], "chan")
    pooled = jnp.moveaxis(pooled_in, 0, 2).reshape(tiles, out_share, half * half)
    w_sum = jnp.sum(w_back.astype(F32), axis=(0, 1))

    g = grad_in.astype(F32)
    main = jnp.moveaxis(g[:, :, :, :rows, :], 0, 2).reshape(tiles, share, S, S + 2)
    extra = jnp.pad(g[:, :, :, rows:, :], ((0, 0), (0, 0), (0, 0), (0, rows - 2), (0, 0)))
    extra = jnp.moveaxis(extra, 0, 2).reshape(tiles, share, S, S + 2)
    grad_padded = jnp.pad(main, ((0, 0), (0, 0), (0, 2), (0, 0))) + jnp.pad(
        extra, ((0, 0), (0, 0), (rows, 0), (0, 0))
    )[:, :, : S + 2, :]

    rims = rim_strips(grad_padded)
    w_len = w_sum.shape[0]
    piece = -(-w_len // n_space)
    w_pieces = jnp.pad(w_sum, (0, piece * n_space - w_len)).reshape(n_space, piece)
    rims_all, w_got = exchange([to_all(rims, n_space), w_pieces], "space")
    w_mine = jnp.sum(w_got, axis=0)
    (w_all,) = exchange([to_all(w_mine, n_space)], "space")
    w_total = w_all.reshape(-1)[:w_len].reshape(out_share, conv_cols + down_cols)

    returned = bordering(rims_all.reshape((n_space * tiles,) + rims.shape[1:]), partner, orientation)
    features_grad = add_edges(grad_padded[:, :, 1:-1, 1:-1], returned).astype(BF16)
    features_grad = features_grad.reshape(tiles, share, S * S)
    grad_scale = float(n_space * tiles * S * S) ** (-0.5)
    conv_grad = w_total[:, :conv_cols].reshape(conv_weight.shape) * grad_scale
    down_grad = w_total[:, conv_cols:].reshape(down_weight.shape) * grad_scale
    return (pooled, features_grad, conv_grad, down_grad)


def solution(mesh):
    placed = (
        P("space", "chan", None),
        P("chan", None, None),
        P("chan", None, None),
        P("space", "chan", None),
        P("space", None),
        P("space", None),
    )
    return jax.shard_map(
        shards,
        mesh=mesh,
        in_specs=placed,
        out_specs=(
            P("space", "chan", None),
            P("space", "chan", None),
            P("chan", None, None),
            P("chan", None, None),
        ),
        check_vma=False,
    )
```

```python
import jax
import jax.numpy as jnp
from jax import lax
from jax.sharding import PartitionSpec as P

S = 64
F32 = jnp.float32
BF16 = jnp.bfloat16


def edge_strips(values):
    return jnp.stack(
        [values[..., 0, :], values[..., :, -1], values[..., -1, :], values[..., :, 0]], axis=-3
    )


def rim_strips(padded):
    return jnp.stack(
        [padded[..., 0, 1:-1], padded[..., 1:-1, -1], padded[..., -1, 1:-1], padded[..., 1:-1, 0]],
        axis=-3,
    )


def bordering(strips, partner, orientation):
    flat = strips.reshape((-1,) + strips.shape[2:])
    picked = jnp.take(flat, partner.reshape(-1), axis=0)
    picked = picked.reshape(partner.shape + strips.shape[2:])
    return jnp.where((orientation == 1)[..., None, None], picked[..., ::-1], picked)


def pad_tile(values, halo_strips):
    tile_side = values.shape[-1]
    widths = [(0, 0)] * (values.ndim - 2) + [(1, 1), (1, 1)]
    padded = jnp.pad(values, widths)
    padded = padded.at[..., 0, 1 : tile_side + 1].set(halo_strips[..., 0, :, :])
    padded = padded.at[..., 1 : tile_side + 1, tile_side + 1].set(halo_strips[..., 1, :, :])
    padded = padded.at[..., tile_side + 1, 1 : tile_side + 1].set(halo_strips[..., 2, :, :])
    return padded.at[..., 1 : tile_side + 1, 0].set(halo_strips[..., 3, :, :])


def pad_cat(values, halo):
    zero = jnp.zeros(values.shape[:2] + (1, 1), values.dtype)
    top = jnp.concatenate([zero, halo[:, 0, :, None, :], zero], axis=3)
    bottom = jnp.concatenate([zero, halo[:, 2, :, None, :], zero], axis=3)
    middle = jnp.concatenate([halo[:, 3, :, :, None], values, halo[:, 1, :, :, None]], axis=3)
    return jnp.concatenate([top, middle, bottom], axis=2)


def add_edges(interior, returned):
    n = interior.shape[-1]
    none = ((0, 0), (0, 0))
    rows = jnp.pad(returned[:, 0, :, None, :], none + ((0, n - 1), (0, 0))) + jnp.pad(
        returned[:, 2, :, None, :], none + ((n - 1, 0), (0, 0))
    )
    cols = jnp.pad(returned[:, 3, :, :, None], none + ((0, 0), (0, n - 1))) + jnp.pad(
        returned[:, 1, :, :, None], none + ((0, 0), (n - 1, 0))
    )
    return interior + (rows + cols)


def unfold(padded, height, width):
    taps = [
        padded[..., row_shift : row_shift + height, col_shift : col_shift + width]
        for row_shift in range(3)
        for col_shift in range(3)
    ]
    return jnp.stack(taps, axis=-4)


def fold_taps(taps):
    total = None
    for row_shift in range(3):
        for col_shift in range(3):
            piece = taps[..., 3 * row_shift + col_shift, :, :, :]
            widths = [(0, 0)] * (piece.ndim - 2) + [
                (row_shift, 2 - row_shift),
                (col_shift, 2 - col_shift),
            ]
            placed = jnp.pad(piece, widths)
            total = placed if total is None else total + placed
    return total


def silu_grad(values):
    gate = jax.nn.sigmoid(values)
    return gate * (1.0 + values * (1.0 - gate))


def exchange(parts, axis):
    count = parts[0].shape[0]
    flat = [p.reshape(count, -1) for p in parts]
    sizes = [f.shape[1] for f in flat]
    total = sum(sizes)
    lanes = -(-total // 128) * 128
    buf = jnp.concatenate(flat + [jnp.zeros((count, lanes - total), flat[0].dtype)], axis=1)
    got = lax.all_to_all(buf.reshape(count, lanes // 128, 128), axis, 0, 0, tiled=True)
    got = got.reshape(count, lanes)
    out, start = [], 0
    for p, size in zip(parts, sizes):
        out.append(got[:, start : start + size].reshape(p.shape))
        start += size
    return out


def to_all(value, count):
    return jnp.broadcast_to(value[None], (count,) + value.shape)


def split_wide(value):
    high = lax.reduce_precision(value, exponent_bits=8, mantissa_bits=7)
    return jnp.stack([high, value - high], axis=1).astype(BF16)


def shards(features, conv_weight, down_weight, cotangent, partner, orientation):
    tiles, share, _ = features.shape
    n_chan = lax.axis_size("chan")
    n_space = lax.axis_size("space")
    in_channels = share * n_chan
    out_share = conv_weight.shape[0]
    out_channels = out_share * n_chan
    rows = S // n_chan
    half = S // 2
    conv_cols = conv_weight.shape[1] * conv_weight.shape[2]
    down_cols = down_weight.shape[1] * down_weight.shape[2]

    weights = jnp.concatenate(
        [conv_weight.reshape(out_share, conv_cols), down_weight.reshape(out_share, down_cols)], axis=1
    )

    images = features.reshape(tiles, share, S, S)
    strips = edge_strips(images)
    (strips_all,) = exchange([to_all(strips, n_space)], "space")
    halo = bordering(strips_all.reshape((n_space * tiles,) + strips.shape[1:]), partner, orientation)
    padded = pad_cat(images, halo)

    bands = jnp.stack([padded[:, :, rows * b : rows * b + rows + 2, :] for b in range(n_chan)])
    cot_bands = jnp.moveaxis(cotangent.reshape(tiles, out_share, n_chan, rows // 2 * half), 2, 0)
    band_in, cot_in, w_in = exchange([bands, cot_bands, to_all(weights, n_chan)], "chan")
    block = jnp.moveaxis(band_in, 0, 1).reshape(tiles, in_channels, rows + 2, S + 2)
    grad_band = jnp.moveaxis(cot_in, 0, 1).reshape(tiles, out_channels, rows // 2, half)
    w_full = w_in.reshape(out_channels, conv_cols + down_cols)
    conv_full = w_full[:, :conv_cols].reshape(out_channels, 9, in_channels)
    down_full = w_full[:, conv_cols:].reshape(out_channels, 4, out_channels)

    plain = ("NCHW", "OIHW", "NCHW")
    swapped = ("CNHW", "IOHW", "NCHW")
    w_conv = conv_full.reshape(out_channels, 3, 3, in_channels).transpose(0, 3, 1, 2)
    w_down = down_full.reshape(out_channels, 2, 2, out_channels).transpose(0, 3, 1, 2)
    pre_act = lax.conv_general_dilated(
        block, w_conv, (1, 1), "VALID", dimension_numbers=plain, preferred_element_type=F32
    )
    activated = jax.nn.silu(pre_act).astype(BF16)
    pooled_rows = lax.conv_general_dilated(
        activated, w_down, (2, 2), "VALID", dimension_numbers=plain, preferred_element_type=F32
    ).astype(BF16)
    down_part = lax.conv_general_dilated(
        activated, grad_band, (1, 1), "VALID", rhs_dilation=(2, 2),
        dimension_numbers=swapped, preferred_element_type=F32,
    )
    down_part = down_part.transpose(1, 2, 3, 0).reshape(out_channels, down_cols)
    w_up = jnp.flip(w_down, (2, 3)).transpose(1, 0, 2, 3)
    grad_act = lax.conv_general_dilated(
        grad_band, w_up, (1, 1), ((1, 1), (1, 1)), lhs_dilation=(2, 2),
        dimension_numbers=plain, preferred_element_type=F32,
    )
    grad_pre = (grad_act * silu_grad(pre_act)).astype(BF16)
    conv_part = lax.conv_general_dilated(
        block, grad_pre, (1, 1), "VALID", dimension_numbers=swapped, preferred_element_type=F32
    )
    conv_part = conv_part.transpose(1, 2, 3, 0).reshape(out_channels, conv_cols)
    w_back_conv = jnp.flip(w_conv, (2, 3)).transpose(1, 0, 2, 3)
    grad_block = lax.conv_general_dilated(
        grad_pre, w_back_conv, (1, 1), ((2, 2), (2, 2)), dimension_numbers=plain,
        preferred_element_type=F32,
    )

    pooled_out = jnp.moveaxis(pooled_rows.reshape(tiles, n_chan, out_share, rows // 2 * half), 1, 0)
    grad_out = jnp.moveaxis(
        grad_block.astype(BF16).reshape(tiles, n_chan, share, rows + 2, S + 2), 1, 0
    )
    w_part = jnp.concatenate([conv_part, down_part], axis=1)
    w_part = split_wide(w_part.reshape(n_chan, out_share * (conv_cols + down_cols)))
    pooled_in, grad_in, w_back = exchange([pooled_out, grad_out, w_part], "chan")
    pooled = jnp.moveaxis(pooled_in, 0, 2).reshape(tiles, out_share, half * half)
    w_sum = jnp.sum(w_back.astype(F32), axis=(0, 1))

    g = grad_in.astype(F32)
    main = jnp.moveaxis(g[:, :, :, :rows, :], 0, 2).reshape(tiles, share, S, S + 2)
    extra = jnp.pad(g[:, :, :, rows:, :], ((0, 0), (0, 0), (0, 0), (0, rows - 2), (0, 0)))
    extra = jnp.moveaxis(extra, 0, 2).reshape(tiles, share, S, S + 2)
    grad_padded = jnp.pad(main, ((0, 0), (0, 0), (0, 2), (0, 0))) + jnp.pad(
        extra, ((0, 0), (0, 0), (rows, 0), (0, 0))
    )[:, :, : S + 2, :]

    rims = rim_strips(grad_padded)
    w_len = w_sum.shape[0]
    piece = -(-w_len // n_space)
    w_pieces = jnp.pad(w_sum, (0, piece * n_space - w_len)).reshape(n_space, piece)
    rims_all, w_got = exchange([to_all(rims.astype(BF16), n_space), split_wide(w_pieces)], "space")
    w_mine = jnp.sum(w_got.astype(F32), axis=(0, 1))
    (w_all,) = exchange([to_all(w_mine, n_space)], "space")
    w_total = w_all.reshape(-1)[:w_len].reshape(out_share, conv_cols + down_cols)

    returned = bordering(rims_all.reshape((n_space * tiles,) + rims.shape[1:]), partner, orientation)
    returned = returned.astype(F32)
    features_grad = add_edges(grad_padded[:, :, 1:-1, 1:-1], returned).astype(BF16)
    features_grad = features_grad.reshape(tiles, share, S * S)
    grad_scale = float(n_space * tiles * S * S) ** (-0.5)
    conv_grad = w_total[:, :conv_cols].reshape(conv_weight.shape) * grad_scale
    down_grad = w_total[:, conv_cols:].reshape(down_weight.shape) * grad_scale
    return (pooled, features_grad, conv_grad, down_grad)


def solution(mesh):
    placed = (
        P("space", "chan", None),
        P("chan", None, None),
        P("chan", None, None),
        P("space", "chan", None),
        P("space", None),
        P("space", None),
    )
    return jax.shard_map(
        shards,
        mesh=mesh,
        in_specs=placed,
        out_specs=(
            P("space", "chan", None),
            P("space", "chan", None),
            P("chan", None, None),
            P("chan", None, None),
        ),
        check_vma=False,
    )
```

```python
import functools

import jax
import jax.numpy as jnp
from jax import lax
from jax.experimental import pallas as pl
from jax.experimental.pallas import tpu as pltpu
from jax.sharding import PartitionSpec as P

S = 64
F32 = jnp.float32
BF16 = jnp.bfloat16


def edge_strips(values):
    return jnp.stack(
        [values[..., 0, :], values[..., :, -1], values[..., -1, :], values[..., :, 0]], axis=-3
    )


def rim_strips(padded):
    return jnp.stack(
        [padded[..., 0, 1:-1], padded[..., 1:-1, -1], padded[..., -1, 1:-1], padded[..., 1:-1, 0]],
        axis=-3,
    )


def bordering(strips, partner, orientation):
    flat = strips.reshape((-1,) + strips.shape[2:])
    picked = jnp.take(flat, partner.reshape(-1), axis=0)
    picked = picked.reshape(partner.shape + strips.shape[2:])
    return jnp.where((orientation == 1)[..., None, None], picked[..., ::-1], picked)


def pad_tile(values, halo_strips):
    tile_side = values.shape[-1]
    widths = [(0, 0)] * (values.ndim - 2) + [(1, 1), (1, 1)]
    padded = jnp.pad(values, widths)
    padded = padded.at[..., 0, 1 : tile_side + 1].set(halo_strips[..., 0, :, :])
    padded = padded.at[..., 1 : tile_side + 1, tile_side + 1].set(halo_strips[..., 1, :, :])
    padded = padded.at[..., tile_side + 1, 1 : tile_side + 1].set(halo_strips[..., 2, :, :])
    return padded.at[..., 1 : tile_side + 1, 0].set(halo_strips[..., 3, :, :])


def pad_cat(values, halo):
    zero = jnp.zeros(values.shape[:2] + (1, 1), values.dtype)
    top = jnp.concatenate([zero, halo[:, 0, :, None, :], zero], axis=3)
    bottom = jnp.concatenate([zero, halo[:, 2, :, None, :], zero], axis=3)
    middle = jnp.concatenate([halo[:, 3, :, :, None], values, halo[:, 1, :, :, None]], axis=3)
    return jnp.concatenate([top, middle, bottom], axis=2)


def add_edges(interior, returned):
    n = interior.shape[-1]
    none = ((0, 0), (0, 0))
    rows = jnp.pad(returned[:, 0, :, None, :], none + ((0, n - 1), (0, 0))) + jnp.pad(
        returned[:, 2, :, None, :], none + ((n - 1, 0), (0, 0))
    )
    cols = jnp.pad(returned[:, 3, :, :, None], none + ((0, 0), (0, n - 1))) + jnp.pad(
        returned[:, 1, :, :, None], none + ((0, 0), (n - 1, 0))
    )
    return interior + (rows + cols)


def unfold(padded, height, width):
    taps = [
        padded[..., row_shift : row_shift + height, col_shift : col_shift + width]
        for row_shift in range(3)
        for col_shift in range(3)
    ]
    return jnp.stack(taps, axis=-4)


def fold_taps(taps):
    total = None
    for row_shift in range(3):
        for col_shift in range(3):
            piece = taps[..., 3 * row_shift + col_shift, :, :, :]
            widths = [(0, 0)] * (piece.ndim - 2) + [
                (row_shift, 2 - row_shift),
                (col_shift, 2 - col_shift),
            ]
            placed = jnp.pad(piece, widths)
            total = placed if total is None else total + placed
    return total


def silu_grad(values):
    gate = jax.nn.sigmoid(values)
    return gate * (1.0 + values * (1.0 - gate))


def exchange(parts, axis):
    count = parts[0].shape[0]
    flat = [p.reshape(count, -1) for p in parts]
    sizes = [f.shape[1] for f in flat]
    total = sum(sizes)
    lanes = -(-total // 128) * 128
    buf = jnp.concatenate(flat + [jnp.zeros((count, lanes - total), flat[0].dtype)], axis=1)
    got = lax.all_to_all(buf.reshape(count, lanes // 128, 128), axis, 0, 0, tiled=True)
    got = got.reshape(count, lanes)
    out, start = [], 0
    for p, size in zip(parts, sizes):
        out.append(got[:, start : start + size].reshape(p.shape))
        start += size
    return out


def to_all(value, count):
    return jnp.broadcast_to(value[None], (count,) + value.shape)


def split_wide(value):
    high = lax.reduce_precision(value, exponent_bits=8, mantissa_bits=7)
    return jnp.stack([high, value - high], axis=1).astype(BF16)


def band_kernel(rows, width, x_ref, cot_ref, wc_ref, wct_ref, wd_ref, wdt_ref, pooled_ref, grad_ref, cg_ref, dg_ref, gpad_ref):
    tiles = x_ref.shape[0]
    span = rows * width
    half = (width - 2) // 2
    offs = [i * width + j for i in range(3) for j in range(3)]
    m = lax.broadcasted_iota(jnp.int32, (span, pooled_ref.shape[2]), 0)
    n = lax.broadcasted_iota(jnp.int32, (span, pooled_ref.shape[2]), 1)
    sels = []
    for p in range(2):
        for q in range(2):
            target = (2 * (n // half) + p) * width + 2 * (n % half) + q
            sels.append(jnp.where(m == target, 1.0, 0.0).astype(BF16))
    cout, cin, lanes = wc_ref.shape[1], wc_ref.shape[2], x_ref.shape[2]
    cg = [jnp.zeros((cout, cin), F32) for _ in range(9)]
    dg = [jnp.zeros((cout, cout), F32) for _ in range(4)]
    nt = (((1,), (1,)), ((), ()))
    gpad_ref[...] = jnp.zeros(gpad_ref.shape, gpad_ref.dtype)
    for t in range(tiles):
        xs = [x_ref[t, :, o:o + span] for o in offs]
        pre = jnp.zeros((cout, span), F32)
        for k in range(9):
            pre = pre + jnp.dot(wc_ref[k], xs[k], preferred_element_type=F32)
        gate = jax.nn.sigmoid(pre)
        act = (pre * gate).astype(BF16)
        cot = cot_ref[t]
        pooled = jnp.zeros(pooled_ref.shape[1:], F32)
        gact = jnp.zeros((cout, span), F32)
        for k in range(4):
            picked = jnp.dot(act, sels[k], preferred_element_type=F32).astype(BF16)
            pooled = pooled + jnp.dot(wd_ref[k], picked, preferred_element_type=F32)
            dg[k] = dg[k] + lax.dot_general(cot, picked, nt, preferred_element_type=F32)
            spread = lax.dot_general(cot, sels[k], nt, preferred_element_type=F32).astype(BF16)
            gact = gact + jnp.dot(wdt_ref[k], spread, preferred_element_type=F32)
        pooled_ref[t] = pooled.astype(BF16)
        gpre = (gact * (gate * (1.0 + pre * (1.0 - gate)))).astype(BF16)
        for k in range(9):
            cg[k] = cg[k] + lax.dot_general(gpre, xs[k], nt, preferred_element_type=F32)
        gpad_ref[:, 256:256 + span] = gpre
        total = jnp.zeros((cin, lanes), F32)
        for k in range(9):
            total = total + jnp.dot(wct_ref[k], gpad_ref[:, 256 - offs[k]:256 - offs[k] + lanes], preferred_element_type=F32)
        grad_ref[t] = total.astype(grad_ref.dtype)
    for k in range(9):
        cg_ref[k] = cg[k]
    for k in range(4):
        dg_ref[k] = dg[k]

def band_call(rows, width, x, cot, wc, wct, wd, wdt):
    tiles, cin, lanes = x.shape
    cout = wc.shape[1]
    vm = pl.BlockSpec(memory_space=pltpu.VMEM)
    return pl.pallas_call(
        functools.partial(band_kernel, rows, width),
        out_shape=(
            jax.ShapeDtypeStruct((tiles, cout, cot.shape[2]), BF16),
            jax.ShapeDtypeStruct((tiles, cin, lanes), BF16),
            jax.ShapeDtypeStruct((9, cout, cin), F32),
            jax.ShapeDtypeStruct((4, cout, cout), F32),
        ),
        in_specs=[vm] * 6,
        out_specs=(vm, vm, vm, vm),
        scratch_shapes=[pltpu.VMEM((cout, lanes + 256), BF16)],
    )(x, cot, wc, wct, wd, wdt)


def shards(features, conv_weight, down_weight, cotangent, partner, orientation):
    tiles, share, _ = features.shape
    n_chan = lax.axis_size("chan")
    n_space = lax.axis_size("space")
    in_channels = share * n_chan
    out_share = conv_weight.shape[0]
    out_channels = out_share * n_chan
    rows = S // n_chan
    half = S // 2
    conv_cols = conv_weight.shape[1] * conv_weight.shape[2]
    down_cols = down_weight.shape[1] * down_weight.shape[2]

    weights = jnp.concatenate(
        [conv_weight.reshape(out_share, conv_cols), down_weight.reshape(out_share, down_cols)], axis=1
    )

    images = features.reshape(tiles, share, S, S)
    strips = edge_strips(images)
    (strips_all,) = exchange([to_all(strips, n_space)], "space")
    halo = bordering(strips_all.reshape((n_space * tiles,) + strips.shape[1:]), partner, orientation)
    padded = pad_cat(images, halo)

    bands = jnp.stack([padded[:, :, rows * b : rows * b + rows + 2, :] for b in range(n_chan)])
    cot_bands = jnp.moveaxis(cotangent.reshape(tiles, out_share, n_chan, rows // 2 * half), 2, 0)
    band_in, cot_in, w_in = exchange([bands, cot_bands, to_all(weights, n_chan)], "chan")
    width = S + 2
    grid = (rows + 2) * width
    lanes = -(-(grid + 2 * width + 2) // 128) * 128
    block = jnp.moveaxis(band_in, 0, 1).reshape(tiles, in_channels, grid)
    block = jnp.pad(block, ((0, 0), (0, 0), (0, lanes - grid)))
    grad_band = jnp.moveaxis(cot_in, 0, 1).reshape(tiles, out_channels, rows // 2 * half)
    w_full = w_in.reshape(out_channels, conv_cols + down_cols)
    conv_full = w_full[:, :conv_cols].reshape(out_channels, 9, in_channels)
    down_full = w_full[:, conv_cols:].reshape(out_channels, 4, out_channels)
    pooled_rows, grad_flat, conv_taps, down_taps = band_call(
        rows, width, block, grad_band,
        conv_full.transpose(1, 0, 2), conv_full.transpose(1, 2, 0),
        down_full.transpose(1, 0, 2), down_full.transpose(1, 2, 0),
    )
    conv_part = conv_taps.transpose(1, 0, 2).reshape(out_channels, conv_cols)
    down_part = down_taps.transpose(1, 0, 2).reshape(out_channels, down_cols)
    grad_block = grad_flat[:, :, :grid].reshape(tiles, in_channels, rows + 2, width)

    pooled_out = jnp.moveaxis(pooled_rows.reshape(tiles, n_chan, out_share, rows // 2 * half), 1, 0)
    grad_out = jnp.moveaxis(
        grad_block.reshape(tiles, n_chan, share, rows + 2, S + 2), 1, 0
    )
    w_part = jnp.concatenate([conv_part, down_part], axis=1)
    w_part = split_wide(w_part.reshape(n_chan, out_share * (conv_cols + down_cols)))
    pooled_in, grad_in, w_back = exchange([pooled_out, grad_out, w_part], "chan")
    pooled = jnp.moveaxis(pooled_in, 0, 2).reshape(tiles, out_share, half * half)
    w_sum = jnp.sum(w_back.astype(F32), axis=(0, 1))

    g = grad_in.astype(F32)
    main = jnp.moveaxis(g[:, :, :, :rows, :], 0, 2).reshape(tiles, share, S, S + 2)
    extra = jnp.pad(g[:, :, :, rows:, :], ((0, 0), (0, 0), (0, 0), (0, rows - 2), (0, 0)))
    extra = jnp.moveaxis(extra, 0, 2).reshape(tiles, share, S, S + 2)
    grad_padded = jnp.pad(main, ((0, 0), (0, 0), (0, 2), (0, 0))) + jnp.pad(
        extra, ((0, 0), (0, 0), (rows, 0), (0, 0))
    )[:, :, : S + 2, :]

    rims = rim_strips(grad_padded)
    w_len = w_sum.shape[0]
    piece = -(-w_len // n_space)
    w_pieces = jnp.pad(w_sum, (0, piece * n_space - w_len)).reshape(n_space, piece)
    rims_all, w_got = exchange([to_all(rims.astype(BF16), n_space), split_wide(w_pieces)], "space")
    w_mine = jnp.sum(w_got.astype(F32), axis=(0, 1))
    (w_all,) = exchange([to_all(w_mine, n_space)], "space")
    w_total = w_all.reshape(-1)[:w_len].reshape(out_share, conv_cols + down_cols)

    returned = bordering(rims_all.reshape((n_space * tiles,) + rims.shape[1:]), partner, orientation)
    returned = returned.astype(F32)
    features_grad = add_edges(grad_padded[:, :, 1:-1, 1:-1], returned).astype(BF16)
    features_grad = features_grad.reshape(tiles, share, S * S)
    grad_scale = float(n_space * tiles * S * S) ** (-0.5)
    conv_grad = w_total[:, :conv_cols].reshape(conv_weight.shape) * grad_scale
    down_grad = w_total[:, conv_cols:].reshape(down_weight.shape) * grad_scale
    return (pooled, features_grad, conv_grad, down_grad)


def solution(mesh):
    placed = (
        P("space", "chan", None),
        P("chan", None, None),
        P("chan", None, None),
        P("space", "chan", None),
        P("space", None),
        P("space", None),
    )
    return jax.shard_map(
        shards,
        mesh=mesh,
        in_specs=placed,
        out_specs=(
            P("space", "chan", None),
            P("space", "chan", None),
            P("chan", None, None),
            P("chan", None, None),
        ),
        check_vma=False,
    )
```

```python
import jax
import jax.numpy as jnp
from jax import lax
from jax.sharding import PartitionSpec as P

S = 64
F32 = jnp.float32
BF16 = jnp.bfloat16


def edge_strips(values):
    return jnp.stack(
        [values[..., 0, :], values[..., :, -1], values[..., -1, :], values[..., :, 0]], axis=-3
    )


def rim_strips(padded):
    return jnp.stack(
        [padded[..., 0, 1:-1], padded[..., 1:-1, -1], padded[..., -1, 1:-1], padded[..., 1:-1, 0]],
        axis=-3,
    )


def bordering(strips, partner, orientation):
    flat = strips.reshape((-1,) + strips.shape[2:])
    picked = jnp.take(flat, partner.reshape(-1), axis=0)
    picked = picked.reshape(partner.shape + strips.shape[2:])
    return jnp.where((orientation == 1)[..., None, None], picked[..., ::-1], picked)


def pad_tile(values, halo_strips):
    tile_side = values.shape[-1]
    widths = [(0, 0)] * (values.ndim - 2) + [(1, 1), (1, 1)]
    padded = jnp.pad(values, widths)
    padded = padded.at[..., 0, 1 : tile_side + 1].set(halo_strips[..., 0, :, :])
    padded = padded.at[..., 1 : tile_side + 1, tile_side + 1].set(halo_strips[..., 1, :, :])
    padded = padded.at[..., tile_side + 1, 1 : tile_side + 1].set(halo_strips[..., 2, :, :])
    return padded.at[..., 1 : tile_side + 1, 0].set(halo_strips[..., 3, :, :])


def pad_cat(values, halo):
    zero = jnp.zeros(values.shape[:2] + (1, 1), values.dtype)
    top = jnp.concatenate([zero, halo[:, 0, :, None, :], zero], axis=3)
    bottom = jnp.concatenate([zero, halo[:, 2, :, None, :], zero], axis=3)
    middle = jnp.concatenate([halo[:, 3, :, :, None], values, halo[:, 1, :, :, None]], axis=3)
    return jnp.concatenate([top, middle, bottom], axis=2)


def add_edges(interior, returned):
    n = interior.shape[-1]
    none = ((0, 0), (0, 0))
    rows = jnp.pad(returned[:, 0, :, None, :], none + ((0, n - 1), (0, 0))) + jnp.pad(
        returned[:, 2, :, None, :], none + ((n - 1, 0), (0, 0))
    )
    cols = jnp.pad(returned[:, 3, :, :, None], none + ((0, 0), (0, n - 1))) + jnp.pad(
        returned[:, 1, :, :, None], none + ((0, 0), (n - 1, 0))
    )
    return interior + (rows + cols)


def unfold(padded, height, width):
    taps = [
        padded[..., row_shift : row_shift + height, col_shift : col_shift + width]
        for row_shift in range(3)
        for col_shift in range(3)
    ]
    return jnp.stack(taps, axis=-4)


def fold_taps(taps):
    total = None
    for row_shift in range(3):
        for col_shift in range(3):
            piece = taps[..., 3 * row_shift + col_shift, :, :, :]
            widths = [(0, 0)] * (piece.ndim - 2) + [
                (row_shift, 2 - row_shift),
                (col_shift, 2 - col_shift),
            ]
            placed = jnp.pad(piece, widths)
            total = placed if total is None else total + placed
    return total


def silu_grad(values):
    gate = jax.nn.sigmoid(values)
    return gate * (1.0 + values * (1.0 - gate))


def exchange(parts, axis):
    count = parts[0].shape[0]
    tile = 4096 // parts[0].dtype.itemsize
    flat = []
    for i, p in enumerate(parts):
        size = p[0].size
        step = 128 if i == len(parts) - 1 else tile
        padded = jnp.pad(p.reshape(count, size), ((0, 0), (0, -size % step)))
        flat.append(padded.reshape(count, -1, 128))
    got = lax.all_to_all(jnp.concatenate(flat, axis=1), axis, 0, 0, tiled=True)
    out, start = [], 0
    for p, f in zip(parts, flat):
        piece = got[:, start : start + f.shape[1]].reshape(count, -1)
        out.append(piece[:, : p[0].size].reshape(p.shape))
        start += f.shape[1]
    return out


def to_all(value, count):
    return jnp.broadcast_to(value[None], (count,) + value.shape)


def split_wide(value):
    high = lax.reduce_precision(value, exponent_bits=8, mantissa_bits=7)
    return jnp.stack([high, value - high], axis=1).astype(BF16)


def shards(features, conv_weight, down_weight, cotangent, partner, orientation):
    tiles, share, _ = features.shape
    n_chan = lax.axis_size("chan")
    n_space = lax.axis_size("space")
    in_channels = share * n_chan
    out_share = conv_weight.shape[0]
    out_channels = out_share * n_chan
    rows = S // n_chan
    half = S // 2
    conv_cols = conv_weight.shape[1] * conv_weight.shape[2]
    down_cols = down_weight.shape[1] * down_weight.shape[2]

    weights = jnp.concatenate(
        [conv_weight.reshape(out_share, conv_cols), down_weight.reshape(out_share, down_cols)], axis=1
    )

    images = features.reshape(tiles, share, S, S)
    strips = edge_strips(images)
    (strips_all,) = exchange([to_all(strips, n_space)], "space")
    halo = bordering(strips_all.reshape((n_space * tiles,) + strips.shape[1:]), partner, orientation)
    padded = pad_cat(images, halo)

    bands = jnp.stack([padded[:, :, rows * b : rows * b + rows + 2, :] for b in range(n_chan)])
    cot_bands = jnp.moveaxis(cotangent.reshape(tiles, out_share, n_chan, rows // 2 * half), 2, 0)
    cot_in, w_in, band_in = exchange([cot_bands, to_all(weights, n_chan), bands], "chan")
    block = jnp.moveaxis(band_in, 0, 1).reshape(tiles, in_channels, rows + 2, S + 2)
    grad_band = jnp.moveaxis(cot_in, 0, 1).reshape(tiles, out_channels, rows // 2, half)
    w_full = w_in.reshape(out_channels, conv_cols + down_cols)
    conv_full = w_full[:, :conv_cols].reshape(out_channels, 9, in_channels)
    down_full = w_full[:, conv_cols:].reshape(out_channels, 4, out_channels)

    plain = ("NCHW", "OIHW", "NCHW")
    swapped = ("CNHW", "IOHW", "NCHW")
    w_conv = conv_full.reshape(out_channels, 3, 3, in_channels).transpose(0, 3, 1, 2)
    w_down = down_full.reshape(out_channels, 2, 2, out_channels).transpose(0, 3, 1, 2)
    pre_act = lax.conv_general_dilated(
        block, w_conv, (1, 1), "VALID", dimension_numbers=plain, preferred_element_type=F32
    )
    activated = jax.nn.silu(pre_act).astype(BF16)
    pooled_rows = lax.conv_general_dilated(
        activated, w_down, (2, 2), "VALID", dimension_numbers=plain, preferred_element_type=F32
    ).astype(BF16)
    down_part = lax.conv_general_dilated(
        activated, grad_band, (1, 1), "VALID", rhs_dilation=(2, 2),
        dimension_numbers=swapped, preferred_element_type=F32,
    )
    down_part = down_part.transpose(1, 2, 3, 0).reshape(out_channels, down_cols)
    w_up = jnp.flip(w_down, (2, 3)).transpose(1, 0, 2, 3)
    grad_act = lax.conv_general_dilated(
        grad_band, w_up, (1, 1), ((1, 1), (1, 1)), lhs_dilation=(2, 2),
        dimension_numbers=plain, preferred_element_type=F32,
    )
    grad_pre = (grad_act * silu_grad(pre_act)).astype(BF16)
    conv_part = lax.conv_general_dilated(
        block, grad_pre, (1, 1), "VALID", dimension_numbers=swapped, preferred_element_type=F32
    )
    conv_part = conv_part.transpose(1, 2, 3, 0).reshape(out_channels, conv_cols)
    w_back_conv = jnp.flip(w_conv, (2, 3)).transpose(1, 0, 2, 3)
    grad_block = lax.conv_general_dilated(
        grad_pre, w_back_conv, (1, 1), ((2, 2), (2, 2)), dimension_numbers=plain,
        preferred_element_type=F32,
    )

    pooled_out = jnp.moveaxis(pooled_rows.reshape(tiles, n_chan, out_share, rows // 2 * half), 1, 0)
    grad_out = jnp.moveaxis(
        grad_block.astype(BF16).reshape(tiles, n_chan, share, rows + 2, S + 2), 1, 0
    )
    w_part = jnp.concatenate([conv_part, down_part], axis=1)
    w_part = split_wide(w_part.reshape(n_chan, out_share * (conv_cols + down_cols)))
    pooled_in, w_back, grad_in = exchange([pooled_out, w_part, grad_out], "chan")
    pooled = jnp.moveaxis(pooled_in, 0, 2).reshape(tiles, out_share, half * half)
    w_sum = jnp.sum(w_back.astype(F32), axis=(0, 1))

    g = grad_in.astype(F32)
    main = jnp.moveaxis(g[:, :, :, :rows, :], 0, 2).reshape(tiles, share, S, S + 2)
    extra = jnp.pad(g[:, :, :, rows:, :], ((0, 0), (0, 0), (0, 0), (0, rows - 2), (0, 0)))
    extra = jnp.moveaxis(extra, 0, 2).reshape(tiles, share, S, S + 2)
    grad_padded = jnp.pad(main, ((0, 0), (0, 0), (0, 2), (0, 0))) + jnp.pad(
        extra, ((0, 0), (0, 0), (rows, 0), (0, 0))
    )[:, :, : S + 2, :]

    rims = rim_strips(grad_padded)
    w_len = w_sum.shape[0]
    piece = -(-w_len // n_space)
    w_pieces = jnp.pad(w_sum, (0, piece * n_space - w_len)).reshape(n_space, piece)
    rims_all, w_got = exchange([to_all(rims.astype(BF16), n_space), split_wide(w_pieces)], "space")
    w_mine = jnp.sum(w_got.astype(F32), axis=(0, 1))
    (w_all,) = exchange([to_all(w_mine, n_space)], "space")
    w_total = w_all.reshape(-1)[:w_len].reshape(out_share, conv_cols + down_cols)

    returned = bordering(rims_all.reshape((n_space * tiles,) + rims.shape[1:]), partner, orientation)
    returned = returned.astype(F32)
    features_grad = add_edges(grad_padded[:, :, 1:-1, 1:-1], returned).astype(BF16)
    features_grad = features_grad.reshape(tiles, share, S * S)
    grad_scale = float(n_space * tiles * S * S) ** (-0.5)
    conv_grad = w_total[:, :conv_cols].reshape(conv_weight.shape) * grad_scale
    down_grad = w_total[:, conv_cols:].reshape(down_weight.shape) * grad_scale
    return (pooled, features_grad, conv_grad, down_grad)


def solution(mesh):
    placed = (
        P("space", "chan", None),
        P("chan", None, None),
        P("chan", None, None),
        P("space", "chan", None),
        P("space", None),
        P("space", None),
    )
    return jax.shard_map(
        shards,
        mesh=mesh,
        in_specs=placed,
        out_specs=(
            P("space", "chan", None),
            P("space", "chan", None),
            P("chan", None, None),
            P("chan", None, None),
        ),
        check_vma=False,
    )
```

```python
import jax
import jax.numpy as jnp
from jax import lax
from jax.sharding import PartitionSpec as P

S = 64
F32 = jnp.float32
BF16 = jnp.bfloat16


def edge_strips(values):
    return jnp.stack(
        [values[..., 0, :], values[..., :, -1], values[..., -1, :], values[..., :, 0]], axis=-3
    )


def rim_strips(padded):
    return jnp.stack(
        [padded[..., 0, 1:-1], padded[..., 1:-1, -1], padded[..., -1, 1:-1], padded[..., 1:-1, 0]],
        axis=-3,
    )


def bordering(strips, partner, orientation):
    flat = strips.reshape((-1,) + strips.shape[2:])
    picked = jnp.take(flat, partner.reshape(-1), axis=0)
    picked = picked.reshape(partner.shape + strips.shape[2:])
    return jnp.where((orientation == 1)[..., None, None], picked[..., ::-1], picked)


def pad_tile(values, halo_strips):
    tile_side = values.shape[-1]
    widths = [(0, 0)] * (values.ndim - 2) + [(1, 1), (1, 1)]
    padded = jnp.pad(values, widths)
    padded = padded.at[..., 0, 1 : tile_side + 1].set(halo_strips[..., 0, :, :])
    padded = padded.at[..., 1 : tile_side + 1, tile_side + 1].set(halo_strips[..., 1, :, :])
    padded = padded.at[..., tile_side + 1, 1 : tile_side + 1].set(halo_strips[..., 2, :, :])
    return padded.at[..., 1 : tile_side + 1, 0].set(halo_strips[..., 3, :, :])


def pad_cat(values, halo):
    zero = jnp.zeros(values.shape[:2] + (1, 1), values.dtype)
    top = jnp.concatenate([zero, halo[:, 0, :, None, :], zero], axis=3)
    bottom = jnp.concatenate([zero, halo[:, 2, :, None, :], zero], axis=3)
    middle = jnp.concatenate([halo[:, 3, :, :, None], values, halo[:, 1, :, :, None]], axis=3)
    return jnp.concatenate([top, middle, bottom], axis=2)


def add_edges(interior, returned):
    n = interior.shape[-1]
    none = ((0, 0), (0, 0))
    rows = jnp.pad(returned[:, 0, :, None, :], none + ((0, n - 1), (0, 0))) + jnp.pad(
        returned[:, 2, :, None, :], none + ((n - 1, 0), (0, 0))
    )
    cols = jnp.pad(returned[:, 3, :, :, None], none + ((0, 0), (0, n - 1))) + jnp.pad(
        returned[:, 1, :, :, None], none + ((0, 0), (n - 1, 0))
    )
    return interior + (rows + cols)


def unfold(padded, height, width):
    taps = [
        padded[..., row_shift : row_shift + height, col_shift : col_shift + width]
        for row_shift in range(3)
        for col_shift in range(3)
    ]
    return jnp.stack(taps, axis=-4)


def fold_taps(taps):
    total = None
    for row_shift in range(3):
        for col_shift in range(3):
            piece = taps[..., 3 * row_shift + col_shift, :, :, :]
            widths = [(0, 0)] * (piece.ndim - 2) + [
                (row_shift, 2 - row_shift),
                (col_shift, 2 - col_shift),
            ]
            placed = jnp.pad(piece, widths)
            total = placed if total is None else total + placed
    return total


def silu_grad(values):
    gate = jax.nn.sigmoid(values)
    return gate * (1.0 + values * (1.0 - gate))


def exchange(parts, axis):
    count = parts[0].shape[0]
    tile = 4096 // parts[0].dtype.itemsize
    flat = []
    for i, p in enumerate(parts):
        size = p[0].size
        step = 128 if i == len(parts) - 1 else tile
        padded = jnp.pad(p.reshape(count, size), ((0, 0), (0, -size % step)))
        flat.append(padded.reshape(count, -1, 128))
    got = lax.all_to_all(jnp.concatenate(flat, axis=1), axis, 0, 0, tiled=True)
    out, start = [], 0
    for p, f in zip(parts, flat):
        piece = got[:, start : start + f.shape[1]].reshape(count, -1)
        out.append(piece[:, : p[0].size].reshape(p.shape))
        start += f.shape[1]
    return out


def to_all(value, count):
    return jnp.broadcast_to(value[None], (count,) + value.shape)


def split_wide(value):
    high = lax.reduce_precision(value, exponent_bits=8, mantissa_bits=7)
    return jnp.concatenate([high, value - high], axis=-1).astype(BF16)


def join_wide(value):
    half = value.shape[-1] // 2
    wide = value.astype(F32)
    return wide[..., :half] + wide[..., half:]


def shards(features, conv_weight, down_weight, cotangent, partner, orientation):
    tiles, share, _ = features.shape
    n_chan = lax.axis_size("chan")
    n_space = lax.axis_size("space")
    in_channels = share * n_chan
    out_share = conv_weight.shape[0]
    out_channels = out_share * n_chan
    rows = S // n_chan
    half = S // 2
    conv_cols = conv_weight.shape[1] * conv_weight.shape[2]
    down_cols = down_weight.shape[1] * down_weight.shape[2]

    weights = jnp.concatenate(
        [conv_weight.reshape(out_share, conv_cols), down_weight.reshape(out_share, down_cols)], axis=1
    )

    images = features.reshape(tiles, share, S, S)
    strips = edge_strips(images)
    (strips_all,) = exchange([to_all(strips, n_space)], "space")
    halo = bordering(strips_all.reshape((n_space * tiles,) + strips.shape[1:]), partner, orientation)
    padded = pad_cat(images, halo)

    head = padded[:, :, : S, :].reshape(tiles, share, n_chan, rows, S + 2)
    tail = jnp.pad(padded[:, :, rows:, :], ((0, 0), (0, 0), (0, rows - 2), (0, 0)))
    tail = tail.reshape(tiles, share, n_chan, rows, S + 2)[:, :, :, :2, :]
    bands = jnp.moveaxis(jnp.concatenate([head, tail], axis=3), 2, 0)
    cot_bands = jnp.moveaxis(cotangent.reshape(tiles, out_share, n_chan, rows // 2 * half), 2, 0)
    cot_in, w_in, band_in = exchange([cot_bands, to_all(weights, n_chan), bands], "chan")
    block = jnp.moveaxis(band_in, 0, 1).reshape(tiles, in_channels, rows + 2, S + 2)
    grad_band = jnp.moveaxis(cot_in, 0, 1).reshape(tiles, out_channels, rows // 2, half)
    w_full = w_in.reshape(out_channels, conv_cols + down_cols)
    conv_full = w_full[:, :conv_cols].reshape(out_channels, 9, in_channels)
    down_full = w_full[:, conv_cols:].reshape(out_channels, 4, out_channels)

    plain = ("NCHW", "OIHW", "NCHW")
    swapped = ("CNHW", "IOHW", "NCHW")
    w_conv = conv_full.reshape(out_channels, 3, 3, in_channels).transpose(0, 3, 1, 2)
    w_down = down_full.reshape(out_channels, 2, 2, out_channels).transpose(0, 3, 1, 2)
    pre_act = lax.conv_general_dilated(
        block, w_conv, (1, 1), "VALID", dimension_numbers=plain, preferred_element_type=F32
    )
    activated = jax.nn.silu(pre_act).astype(BF16)
    pooled_rows = lax.conv_general_dilated(
        activated, w_down, (2, 2), "VALID", dimension_numbers=plain, preferred_element_type=F32
    ).astype(BF16)
    down_part = lax.conv_general_dilated(
        activated, grad_band, (1, 1), "VALID", rhs_dilation=(2, 2),
        dimension_numbers=swapped, preferred_element_type=F32,
    )
    down_part = down_part.transpose(1, 2, 3, 0).reshape(out_channels, down_cols)
    w_up = jnp.flip(w_down, (2, 3)).transpose(1, 0, 2, 3)
    grad_act = lax.conv_general_dilated(
        grad_band, w_up, (1, 1), ((1, 1), (1, 1)), lhs_dilation=(2, 2),
        dimension_numbers=plain, preferred_element_type=F32,
    )
    grad_pre = (grad_act * silu_grad(pre_act)).astype(BF16)
    conv_part = lax.conv_general_dilated(
        block, grad_pre, (1, 1), "VALID", dimension_numbers=swapped, preferred_element_type=F32
    )
    conv_part = conv_part.transpose(1, 2, 3, 0).reshape(out_channels, conv_cols)
    w_back_conv = jnp.flip(w_conv, (2, 3)).transpose(1, 0, 2, 3)
    grad_block = lax.conv_general_dilated(
        grad_pre, w_back_conv, (1, 1), ((2, 2), (2, 2)), dimension_numbers=plain,
        preferred_element_type=F32,
    )

    pooled_out = jnp.moveaxis(pooled_rows.reshape(tiles, n_chan, out_share, rows // 2 * half), 1, 0)
    grad_out = jnp.moveaxis(
        grad_block.astype(BF16).reshape(tiles, n_chan, share, rows + 2, S + 2), 1, 0
    )
    w_part = jnp.concatenate([conv_part, down_part], axis=1)
    w_part = split_wide(w_part.reshape(n_chan, out_share * (conv_cols + down_cols)))
    pooled_in, w_back, grad_in = exchange([pooled_out, w_part, grad_out], "chan")
    pooled = jnp.moveaxis(pooled_in, 0, 2).reshape(tiles, out_share, half * half)
    w_sum = jnp.sum(join_wide(w_back), axis=0)

    g = grad_in.astype(F32)
    main = jnp.moveaxis(g[:, :, :, :rows, :], 0, 2).reshape(tiles, share, S, S + 2)
    extra = jnp.pad(g[:, :, :, rows:, :], ((0, 0), (0, 0), (0, 0), (0, rows - 2), (0, 0)))
    extra = jnp.moveaxis(extra, 0, 2).reshape(tiles, share, S, S + 2)
    grad_padded = jnp.pad(main, ((0, 0), (0, 0), (0, 2), (0, 0))) + jnp.pad(
        extra, ((0, 0), (0, 0), (rows, 0), (0, 0))
    )[:, :, : S + 2, :]

    rims = rim_strips(grad_padded)
    w_len = w_sum.shape[0]
    piece = -(-w_len // n_space)
    w_pieces = jnp.pad(w_sum, (0, piece * n_space - w_len)).reshape(n_space, piece)
    rims_all, w_got = exchange([to_all(rims.astype(BF16), n_space), split_wide(w_pieces)], "space")
    w_mine = jnp.sum(join_wide(w_got), axis=0)
    (w_all,) = exchange([to_all(w_mine, n_space)], "space")
    w_total = w_all.reshape(-1)[:w_len].reshape(out_share, conv_cols + down_cols)

    returned = bordering(rims_all.reshape((n_space * tiles,) + rims.shape[1:]), partner, orientation)
    returned = returned.astype(F32)
    features_grad = add_edges(grad_padded[:, :, 1:-1, 1:-1], returned).astype(BF16)
    features_grad = features_grad.reshape(tiles, share, S * S)
    grad_scale = float(n_space * tiles * S * S) ** (-0.5)
    conv_grad = w_total[:, :conv_cols].reshape(conv_weight.shape) * grad_scale
    down_grad = w_total[:, conv_cols:].reshape(down_weight.shape) * grad_scale
    return (pooled, features_grad, conv_grad, down_grad)


def solution(mesh):
    placed = (
        P("space", "chan", None),
        P("chan", None, None),
        P("chan", None, None),
        P("space", "chan", None),
        P("space", None),
        P("space", None),
    )
    return jax.shard_map(
        shards,
        mesh=mesh,
        in_specs=placed,
        out_specs=(
            P("space", "chan", None),
            P("space", "chan", None),
            P("chan", None, None),
            P("chan", None, None),
        ),
        check_vma=False,
    )
```

```python
import jax
import jax.numpy as jnp
from jax import lax
from jax.sharding import PartitionSpec as P

S = 64
F32 = jnp.float32
BF16 = jnp.bfloat16


def edge_strips(values):
    return jnp.stack(
        [values[..., 0, :], values[..., :, -1], values[..., -1, :], values[..., :, 0]], axis=-3
    )


def rim_strips(padded):
    return jnp.stack(
        [padded[..., 0, 1:-1], padded[..., 1:-1, -1], padded[..., -1, 1:-1], padded[..., 1:-1, 0]],
        axis=-3,
    )


def bordering(strips, partner, orientation):
    flat = strips.reshape((-1,) + strips.shape[2:])
    picked = jnp.take(flat, partner.reshape(-1), axis=0)
    picked = picked.reshape(partner.shape + strips.shape[2:])
    return jnp.where((orientation == 1)[..., None, None], picked[..., ::-1], picked)


def pad_tile(values, halo_strips):
    tile_side = values.shape[-1]
    widths = [(0, 0)] * (values.ndim - 2) + [(1, 1), (1, 1)]
    padded = jnp.pad(values, widths)
    padded = padded.at[..., 0, 1 : tile_side + 1].set(halo_strips[..., 0, :, :])
    padded = padded.at[..., 1 : tile_side + 1, tile_side + 1].set(halo_strips[..., 1, :, :])
    padded = padded.at[..., tile_side + 1, 1 : tile_side + 1].set(halo_strips[..., 2, :, :])
    return padded.at[..., 1 : tile_side + 1, 0].set(halo_strips[..., 3, :, :])


def pad_cat(values, halo):
    zero = jnp.zeros(values.shape[:2] + (1, 1), values.dtype)
    top = jnp.concatenate([zero, halo[:, 0, :, None, :], zero], axis=3)
    bottom = jnp.concatenate([zero, halo[:, 2, :, None, :], zero], axis=3)
    middle = jnp.concatenate([halo[:, 3, :, :, None], values, halo[:, 1, :, :, None]], axis=3)
    return jnp.concatenate([top, middle, bottom], axis=2)


def add_edges(interior, returned):
    n = interior.shape[-1]
    none = ((0, 0), (0, 0))
    rows = jnp.pad(returned[:, 0, :, None, :], none + ((0, n - 1), (0, 0))) + jnp.pad(
        returned[:, 2, :, None, :], none + ((n - 1, 0), (0, 0))
    )
    cols = jnp.pad(returned[:, 3, :, :, None], none + ((0, 0), (0, n - 1))) + jnp.pad(
        returned[:, 1, :, :, None], none + ((0, 0), (n - 1, 0))
    )
    return interior + (rows + cols)


def unfold(padded, height, width):
    taps = [
        padded[..., row_shift : row_shift + height, col_shift : col_shift + width]
        for row_shift in range(3)
        for col_shift in range(3)
    ]
    return jnp.stack(taps, axis=-4)


def fold_taps(taps):
    total = None
    for row_shift in range(3):
        for col_shift in range(3):
            piece = taps[..., 3 * row_shift + col_shift, :, :, :]
            widths = [(0, 0)] * (piece.ndim - 2) + [
                (row_shift, 2 - row_shift),
                (col_shift, 2 - col_shift),
            ]
            placed = jnp.pad(piece, widths)
            total = placed if total is None else total + placed
    return total


def silu_grad(values):
    gate = jax.nn.sigmoid(values)
    return gate * (1.0 + values * (1.0 - gate))


def exchange(parts, axis):
    count = parts[0].shape[0]
    tile = 4096 // parts[0].dtype.itemsize
    flat = []
    for i, p in enumerate(parts):
        size = p[0].size
        step = 128 if i == len(parts) - 1 else tile
        padded = jnp.pad(p.reshape(count, size), ((0, 0), (0, -size % step)))
        flat.append(padded.reshape(count, -1, 128))
    got = lax.all_to_all(jnp.concatenate(flat, axis=1), axis, 0, 0, tiled=True)
    out, start = [], 0
    for p, f in zip(parts, flat):
        piece = got[:, start : start + f.shape[1]].reshape(count, -1)
        out.append(piece[:, : p[0].size].reshape(p.shape))
        start += f.shape[1]
    return out


def to_all(value, count):
    return jnp.broadcast_to(value[None], (count,) + value.shape)


def split_wide(value):
    high = lax.reduce_precision(value, exponent_bits=8, mantissa_bits=7)
    return jnp.concatenate([high, value - high], axis=-1).astype(BF16)


def join_wide(value):
    half = value.shape[-1] // 2
    wide = value.astype(F32)
    return wide[..., :half] + wide[..., half:]


def shards(features, conv_weight, down_weight, cotangent, partner, orientation):
    tiles, share, _ = features.shape
    n_chan = lax.axis_size("chan")
    n_space = lax.axis_size("space")
    in_channels = share * n_chan
    out_share = conv_weight.shape[0]
    out_channels = out_share * n_chan
    rows = S // n_chan
    half = S // 2
    conv_cols = conv_weight.shape[1] * conv_weight.shape[2]
    down_cols = down_weight.shape[1] * down_weight.shape[2]

    weights = jnp.concatenate(
        [conv_weight.reshape(out_share, conv_cols), down_weight.reshape(out_share, down_cols)], axis=1
    )

    images = features.reshape(tiles, share, S, S)
    strips = edge_strips(images)
    (strips_all,) = exchange([to_all(strips, n_space)], "space")
    halo = bordering(strips_all.reshape((n_space * tiles,) + strips.shape[1:]), partner, orientation)
    padded = pad_cat(images, halo)

    head = padded[:, :, : S, :].reshape(tiles, share, n_chan, rows, S + 2)
    tail = jnp.pad(padded[:, :, rows:, :], ((0, 0), (0, 0), (0, rows - 2), (0, 0)))
    tail = tail.reshape(tiles, share, n_chan, rows, S + 2)[:, :, :, :2, :]
    bands = jnp.moveaxis(jnp.concatenate([head, tail], axis=3), 2, 0)
    cot_bands = jnp.moveaxis(cotangent.reshape(tiles, out_share, n_chan, rows // 2 * half), 2, 0)
    cot_in, w_in, band_in = exchange([cot_bands, to_all(weights, n_chan), bands], "chan")
    block = jnp.moveaxis(band_in, 0, 1).reshape(tiles, in_channels, rows + 2, S + 2)
    grad_band = jnp.moveaxis(cot_in, 0, 1).reshape(tiles, out_channels, rows // 2, half)
    w_full = w_in.reshape(out_channels, conv_cols + down_cols)
    conv_full = w_full[:, :conv_cols].reshape(out_channels, 9, in_channels)
    down_full = w_full[:, conv_cols:].reshape(out_channels, 4, out_channels)

    plain = ("NCHW", "OIHW", "NCHW")
    swapped = ("CNHW", "IOHW", "NCHW")
    w_conv = conv_full.reshape(out_channels, 3, 3, in_channels).transpose(0, 3, 1, 2)
    w_down = down_full.reshape(out_channels, 2, 2, out_channels).transpose(0, 3, 1, 2)
    pre_act = lax.conv_general_dilated(
        block, w_conv, (1, 1), "VALID", dimension_numbers=plain, preferred_element_type=F32
    )
    activated = jax.nn.silu(pre_act).astype(BF16)
    pooled_rows = lax.conv_general_dilated(
        activated, w_down, (2, 2), "VALID", dimension_numbers=plain, preferred_element_type=F32
    ).astype(BF16)
    down_part = lax.conv_general_dilated(
        activated, grad_band, (1, 1), "VALID", rhs_dilation=(2, 2),
        dimension_numbers=swapped, preferred_element_type=F32,
    )
    down_part = down_part.transpose(1, 2, 3, 0).reshape(out_channels, down_cols)
    w_up = jnp.flip(w_down, (2, 3)).transpose(1, 0, 2, 3)
    grad_act = lax.conv_general_dilated(
        grad_band, w_up, (1, 1), ((1, 1), (1, 1)), lhs_dilation=(2, 2),
        dimension_numbers=plain, preferred_element_type=F32,
    )
    grad_pre = (grad_act * silu_grad(pre_act)).astype(BF16)
    conv_part = lax.conv_general_dilated(
        block, grad_pre, (1, 1), "VALID", dimension_numbers=swapped, preferred_element_type=F32
    )
    conv_part = conv_part.transpose(1, 2, 3, 0).reshape(out_channels, conv_cols)
    w_back_conv = jnp.flip(w_conv, (2, 3)).transpose(1, 0, 2, 3)
    grad_block = lax.conv_general_dilated(
        grad_pre, w_back_conv, (1, 1), ((2, 2), (2, 2)), dimension_numbers=plain,
        preferred_element_type=F32,
    )

    pooled_out = jnp.moveaxis(pooled_rows.reshape(tiles, n_chan, out_share, rows // 2 * half), 1, 0)
    grad_out = jnp.moveaxis(
        grad_block.astype(BF16).reshape(tiles, n_chan, share, rows + 2, S + 2), 1, 0
    )
    w_part = jnp.concatenate([conv_part, down_part], axis=1)
    w_part = split_wide(w_part.reshape(n_chan, out_share * (conv_cols + down_cols)))
    pooled_in, w_back, grad_in = exchange([pooled_out, w_part, grad_out], "chan")
    pooled = jnp.moveaxis(pooled_in, 0, 2).reshape(tiles, out_share, half * half)
    w_sum = jnp.sum(join_wide(w_back), axis=0)

    g = grad_in.astype(F32)

    def assemble(bands_of):
        width = bands_of.shape[-1]
        main = jnp.moveaxis(bands_of[:, :, :, :rows, :], 0, 2).reshape(tiles, share, S, width)
        extra = jnp.pad(bands_of[:, :, :, rows:, :], ((0, 0), (0, 0), (0, 0), (0, rows - 2), (0, 0)))
        extra = jnp.moveaxis(extra, 0, 2).reshape(tiles, share, S, width)
        return jnp.pad(main, ((0, 0), (0, 0), (0, 2), (0, 0))) + jnp.pad(
            extra, ((0, 0), (0, 0), (rows, 0), (0, 0))
        )[:, :, : S + 2, :]

    sides = assemble(jnp.concatenate([g[..., :1], g[..., -1:]], axis=-1))
    rims = jnp.stack(
        [g[0, :, :, 0, 1:-1], sides[:, :, 1:-1, 1], g[-1, :, :, -1, 1:-1], sides[:, :, 1:-1, 0]], axis=1
    )
    w_len = w_sum.shape[0]
    piece = -(-w_len // n_space)
    w_pieces = jnp.pad(w_sum, (0, piece * n_space - w_len)).reshape(n_space, piece)
    rims_all, w_got = exchange([to_all(rims.astype(BF16), n_space), split_wide(w_pieces)], "space")
    w_mine = jnp.sum(join_wide(w_got), axis=0)
    (w_all,) = exchange([to_all(w_mine, n_space)], "space")
    w_total = w_all.reshape(-1)[:w_len].reshape(out_share, conv_cols + down_cols)

    returned = bordering(rims_all.reshape((n_space * tiles,) + rims.shape[1:]), partner, orientation)
    returned = returned.astype(F32)
    features_grad = add_edges(assemble(g)[:, :, 1:-1, 1:-1], returned).astype(BF16)
    features_grad = features_grad.reshape(tiles, share, S * S)
    grad_scale = float(n_space * tiles * S * S) ** (-0.5)
    conv_grad = w_total[:, :conv_cols].reshape(conv_weight.shape) * grad_scale
    down_grad = w_total[:, conv_cols:].reshape(down_weight.shape) * grad_scale
    return (pooled, features_grad, conv_grad, down_grad)


def solution(mesh):
    placed = (
        P("space", "chan", None),
        P("chan", None, None),
        P("chan", None, None),
        P("space", "chan", None),
        P("space", None),
        P("space", None),
    )
    return jax.shard_map(
        shards,
        mesh=mesh,
        in_specs=placed,
        out_specs=(
            P("space", "chan", None),
            P("space", "chan", None),
            P("chan", None, None),
            P("chan", None, None),
        ),
        check_vma=False,
    )
```

```python
import jax
import jax.numpy as jnp
from jax import lax
from jax.sharding import PartitionSpec as P

S = 64
F32 = jnp.float32
BF16 = jnp.bfloat16


def edge_strips(values):
    return jnp.stack(
        [values[..., 0, :], values[..., :, -1], values[..., -1, :], values[..., :, 0]], axis=-3
    )


def rim_strips(padded):
    return jnp.stack(
        [padded[..., 0, 1:-1], padded[..., 1:-1, -1], padded[..., -1, 1:-1], padded[..., 1:-1, 0]],
        axis=-3,
    )


def bordering(strips, partner, orientation):
    flat = strips.reshape((-1,) + strips.shape[2:])
    picked = jnp.take(flat, partner.reshape(-1), axis=0)
    picked = picked.reshape(partner.shape + strips.shape[2:])
    return jnp.where((orientation == 1)[..., None, None], picked[..., ::-1], picked)


def pad_tile(values, halo_strips):
    tile_side = values.shape[-1]
    widths = [(0, 0)] * (values.ndim - 2) + [(1, 1), (1, 1)]
    padded = jnp.pad(values, widths)
    padded = padded.at[..., 0, 1 : tile_side + 1].set(halo_strips[..., 0, :, :])
    padded = padded.at[..., 1 : tile_side + 1, tile_side + 1].set(halo_strips[..., 1, :, :])
    padded = padded.at[..., tile_side + 1, 1 : tile_side + 1].set(halo_strips[..., 2, :, :])
    return padded.at[..., 1 : tile_side + 1, 0].set(halo_strips[..., 3, :, :])


def pad_cat(values, halo):
    zero = jnp.zeros(values.shape[:2] + (1, 1), values.dtype)
    top = jnp.concatenate([zero, halo[:, 0, :, None, :], zero], axis=3)
    bottom = jnp.concatenate([zero, halo[:, 2, :, None, :], zero], axis=3)
    middle = jnp.concatenate([halo[:, 3, :, :, None], values, halo[:, 1, :, :, None]], axis=3)
    return jnp.concatenate([top, middle, bottom], axis=2)


def add_edges(interior, returned):
    n = interior.shape[-1]
    none = ((0, 0), (0, 0))
    rows = jnp.pad(returned[:, 0, :, None, :], none + ((0, n - 1), (0, 0))) + jnp.pad(
        returned[:, 2, :, None, :], none + ((n - 1, 0), (0, 0))
    )
    cols = jnp.pad(returned[:, 3, :, :, None], none + ((0, 0), (0, n - 1))) + jnp.pad(
        returned[:, 1, :, :, None], none + ((0, 0), (n - 1, 0))
    )
    return interior + (rows + cols)


def unfold(padded, height, width):
    taps = [
        padded[..., row_shift : row_shift + height, col_shift : col_shift + width]
        for row_shift in range(3)
        for col_shift in range(3)
    ]
    return jnp.stack(taps, axis=-4)


def fold_taps(taps):
    total = None
    for row_shift in range(3):
        for col_shift in range(3):
            piece = taps[..., 3 * row_shift + col_shift, :, :, :]
            widths = [(0, 0)] * (piece.ndim - 2) + [
                (row_shift, 2 - row_shift),
                (col_shift, 2 - col_shift),
            ]
            placed = jnp.pad(piece, widths)
            total = placed if total is None else total + placed
    return total


def silu_grad(values):
    gate = jax.nn.sigmoid(values)
    return gate * (1.0 + values * (1.0 - gate))


def exchange(parts, axis):
    count = parts[0].shape[0]
    tile = 4096 // parts[0].dtype.itemsize
    flat = []
    for i, p in enumerate(parts):
        size = p[0].size
        step = 128 if i == len(parts) - 1 else tile
        padded = jnp.pad(p.reshape(count, size), ((0, 0), (0, -size % step)))
        flat.append(padded.reshape(count, -1, 128))
    got = lax.all_to_all(jnp.concatenate(flat, axis=1), axis, 0, 0, tiled=True)
    out, start = [], 0
    for p, f in zip(parts, flat):
        piece = got[:, start : start + f.shape[1]].reshape(count, -1)
        out.append(piece[:, : p[0].size].reshape(p.shape))
        start += f.shape[1]
    return out


def to_all(value, count):
    return jnp.broadcast_to(value[None], (count,) + value.shape)


def split_wide(value):
    high = lax.reduce_precision(value, exponent_bits=8, mantissa_bits=7)
    return jnp.concatenate([high, value - high], axis=-1).astype(BF16)


def join_wide(value):
    half = value.shape[-1] // 2
    wide = value.astype(F32)
    return wide[..., :half] + wide[..., half:]


def shards(features, conv_weight, down_weight, cotangent, partner, orientation):
    tiles, share, _ = features.shape
    n_chan = lax.axis_size("chan")
    n_space = lax.axis_size("space")
    in_channels = share * n_chan
    out_share = conv_weight.shape[0]
    out_channels = out_share * n_chan
    rows = S // n_chan
    half = S // 2
    conv_cols = conv_weight.shape[1] * conv_weight.shape[2]
    down_cols = down_weight.shape[1] * down_weight.shape[2]

    weights = jnp.concatenate(
        [conv_weight.reshape(out_share, conv_cols), down_weight.reshape(out_share, down_cols)], axis=1
    )

    images = features.reshape(tiles, share, S, S)
    strips = edge_strips(images)
    (strips_all,) = exchange([to_all(strips, n_space)], "space")
    halo = bordering(strips_all.reshape((n_space * tiles,) + strips.shape[1:]), partner, orientation)
    padded = pad_cat(images, halo)

    head = padded[:, :, : S, :].reshape(tiles, share, n_chan, rows, S + 2)
    tail = jnp.pad(padded[:, :, rows:, :], ((0, 0), (0, 0), (0, rows - 2), (0, 0)))
    tail = tail.reshape(tiles, share, n_chan, rows, S + 2)[:, :, :, :2, :]
    bands = jnp.moveaxis(jnp.concatenate([head, tail], axis=3), 2, 0)
    cot_bands = jnp.moveaxis(cotangent.reshape(tiles, out_share, n_chan, rows // 2 * half), 2, 0)
    cot_in, w_in, band_in = exchange([cot_bands, to_all(weights, n_chan), bands], "chan")
    block = jnp.moveaxis(band_in, 0, 1).reshape(tiles, in_channels, rows + 2, S + 2)
    grad_band = jnp.moveaxis(cot_in, 0, 1).reshape(tiles, out_channels, rows // 2, half)
    w_full = w_in.reshape(out_channels, conv_cols + down_cols)
    conv_full = w_full[:, :conv_cols].reshape(out_channels, 9, in_channels)
    down_full = w_full[:, conv_cols:].reshape(out_channels, 4, out_channels)

    plain = ("NCHW", "OIHW", "NCHW")
    swapped = ("CNHW", "IOHW", "NCHW")
    w_conv = conv_full.reshape(out_channels, 3, 3, in_channels).transpose(0, 3, 1, 2)
    w_down = down_full.reshape(out_channels, 2, 2, out_channels).transpose(0, 3, 1, 2)
    pre_act = lax.conv_general_dilated(
        block, w_conv, (1, 1), "VALID", dimension_numbers=plain, preferred_element_type=F32
    )
    activated = jax.nn.silu(pre_act).astype(BF16)
    pooled_rows = lax.conv_general_dilated(
        activated, w_down, (2, 2), "VALID", dimension_numbers=plain, preferred_element_type=F32
    ).astype(BF16)
    down_part = lax.conv_general_dilated(
        activated, grad_band, (1, 1), "VALID", rhs_dilation=(2, 2),
        dimension_numbers=swapped, preferred_element_type=F32,
    )
    down_part = down_part.transpose(1, 2, 3, 0).reshape(out_channels, down_cols)
    w_up = jnp.flip(w_down, (2, 3)).transpose(1, 0, 2, 3)
    grad_act = lax.conv_general_dilated(
        grad_band, w_up, (1, 1), ((1, 1), (1, 1)), lhs_dilation=(2, 2),
        dimension_numbers=plain, preferred_element_type=F32,
    )
    grad_pre = (grad_act * silu_grad(pre_act)).astype(BF16)
    conv_part = lax.conv_general_dilated(
        block, grad_pre, (1, 1), "VALID", dimension_numbers=swapped, preferred_element_type=F32
    )
    conv_part = conv_part.transpose(1, 2, 3, 0).reshape(out_channels, conv_cols)
    w_back_conv = jnp.flip(w_conv, (2, 3)).transpose(1, 0, 2, 3)
    grad_block = lax.conv_general_dilated(
        grad_pre, w_back_conv, (1, 1), ((2, 2), (2, 2)), dimension_numbers=plain,
        preferred_element_type=F32,
    )

    pooled_out = jnp.moveaxis(pooled_rows.reshape(tiles, n_chan, out_share, rows // 2 * half), 1, 0)
    grad_out = jnp.moveaxis(
        grad_block.astype(BF16).reshape(tiles, n_chan, share, rows + 2, S + 2), 1, 0
    )
    down_dest = down_part.reshape(n_chan, out_share * down_cols)
    conv_dest = conv_part.reshape(n_chan, out_share, 9, in_channels).transpose(0, 2, 1, 3)
    w_part = jnp.concatenate([down_dest, conv_dest.reshape(n_chan, out_share * conv_cols)], axis=1)
    w_part = split_wide(w_part)
    pooled_in, w_back, grad_in = exchange([pooled_out, w_part, grad_out], "chan")
    pooled = jnp.moveaxis(pooled_in, 0, 2).reshape(tiles, out_share, half * half)
    w_sum = jnp.sum(join_wide(w_back), axis=0)

    g = grad_in.astype(F32)
    main = jnp.moveaxis(g[:, :, :, :rows, :], 0, 2).reshape(tiles, share, S, S + 2)
    extra = jnp.pad(g[:, :, :, rows:, :], ((0, 0), (0, 0), (0, 0), (0, rows - 2), (0, 0)))
    extra = jnp.moveaxis(extra, 0, 2).reshape(tiles, share, S, S + 2)
    grad_padded = jnp.pad(main, ((0, 0), (0, 0), (0, 2), (0, 0))) + jnp.pad(
        extra, ((0, 0), (0, 0), (rows, 0), (0, 0))
    )[:, :, : S + 2, :]

    rims = rim_strips(grad_padded)
    w_len = w_sum.shape[0]
    piece = -(-w_len // n_space)
    w_pieces = jnp.pad(w_sum, (0, piece * n_space - w_len)).reshape(n_space, piece)
    rims_all, w_got = exchange([to_all(rims.astype(BF16), n_space), split_wide(w_pieces)], "space")
    grad_scale = float(n_space * tiles * S * S) ** (-0.5)
    w_mine = jnp.sum(join_wide(w_got), axis=0) * grad_scale
    (w_all,) = exchange([to_all(w_mine, n_space)], "space")
    w_total = w_all.reshape(-1)[:w_len]

    returned = bordering(rims_all.reshape((n_space * tiles,) + rims.shape[1:]), partner, orientation)
    returned = returned.astype(F32)
    features_grad = add_edges(grad_padded[:, :, 1:-1, 1:-1], returned).astype(BF16)
    features_grad = features_grad.reshape(tiles, share, S * S)
    down_len = out_share * down_cols
    down_grad = w_total[:down_len].reshape(down_weight.shape)
    conv_grad = w_total[down_len:].reshape(9, out_share, in_channels).transpose(1, 0, 2)
    return (pooled, features_grad, conv_grad, down_grad)


def solution(mesh):
    placed = (
        P("space", "chan", None),
        P("chan", None, None),
        P("chan", None, None),
        P("space", "chan", None),
        P("space", None),
        P("space", None),
    )
    return jax.shard_map(
        shards,
        mesh=mesh,
        in_specs=placed,
        out_specs=(
            P("space", "chan", None),
            P("space", "chan", None),
            P("chan", None, None),
            P("chan", None, None),
        ),
        check_vma=False,
    )
```

```python
import jax
import jax.numpy as jnp
from jax import lax
from jax.sharding import PartitionSpec as P

S = 64
F32 = jnp.float32
BF16 = jnp.bfloat16


def edge_strips(values):
    return jnp.stack(
        [values[..., 0, :], values[..., :, -1], values[..., -1, :], values[..., :, 0]], axis=-3
    )


def rim_strips(padded):
    return jnp.stack(
        [padded[..., 0, 1:-1], padded[..., 1:-1, -1], padded[..., -1, 1:-1], padded[..., 1:-1, 0]],
        axis=-3,
    )


def bordering(strips, partner, orientation):
    flat = strips.reshape((-1,) + strips.shape[2:])
    picked = jnp.take(flat, partner.reshape(-1), axis=0)
    picked = picked.reshape(partner.shape + strips.shape[2:])
    return jnp.where((orientation == 1)[..., None, None], picked[..., ::-1], picked)


def pad_tile(values, halo_strips):
    tile_side = values.shape[-1]
    widths = [(0, 0)] * (values.ndim - 2) + [(1, 1), (1, 1)]
    padded = jnp.pad(values, widths)
    padded = padded.at[..., 0, 1 : tile_side + 1].set(halo_strips[..., 0, :, :])
    padded = padded.at[..., 1 : tile_side + 1, tile_side + 1].set(halo_strips[..., 1, :, :])
    padded = padded.at[..., tile_side + 1, 1 : tile_side + 1].set(halo_strips[..., 2, :, :])
    return padded.at[..., 1 : tile_side + 1, 0].set(halo_strips[..., 3, :, :])


def pad_cat(values, halo):
    zero = jnp.zeros(values.shape[:2] + (1, 1), values.dtype)
    top = jnp.concatenate([zero, halo[:, 0, :, None, :], zero], axis=3)
    bottom = jnp.concatenate([zero, halo[:, 2, :, None, :], zero], axis=3)
    middle = jnp.concatenate([halo[:, 3, :, :, None], values, halo[:, 1, :, :, None]], axis=3)
    return jnp.concatenate([top, middle, bottom], axis=2)


def add_edges(interior, returned):
    n = interior.shape[-1]
    none = ((0, 0), (0, 0))
    rows = jnp.pad(returned[:, 0, :, None, :], none + ((0, n - 1), (0, 0))) + jnp.pad(
        returned[:, 2, :, None, :], none + ((n - 1, 0), (0, 0))
    )
    cols = jnp.pad(returned[:, 3, :, :, None], none + ((0, 0), (0, n - 1))) + jnp.pad(
        returned[:, 1, :, :, None], none + ((0, 0), (n - 1, 0))
    )
    return interior + (rows + cols)


def unfold(padded, height, width):
    taps = [
        padded[..., row_shift : row_shift + height, col_shift : col_shift + width]
        for row_shift in range(3)
        for col_shift in range(3)
    ]
    return jnp.stack(taps, axis=-4)


def fold_taps(taps):
    total = None
    for row_shift in range(3):
        for col_shift in range(3):
            piece = taps[..., 3 * row_shift + col_shift, :, :, :]
            widths = [(0, 0)] * (piece.ndim - 2) + [
                (row_shift, 2 - row_shift),
                (col_shift, 2 - col_shift),
            ]
            placed = jnp.pad(piece, widths)
            total = placed if total is None else total + placed
    return total


def silu_grad(values):
    gate = jax.nn.sigmoid(values)
    return gate * (1.0 + values * (1.0 - gate))


def exchange(parts, axis):
    count = parts[0].shape[0]
    tile = 4096 // parts[0].dtype.itemsize
    flat = []
    for i, p in enumerate(parts):
        size = p[0].size
        step = 128 if i == len(parts) - 1 else tile
        padded = jnp.pad(p.reshape(count, size), ((0, 0), (0, -size % step)))
        flat.append(padded.reshape(count, -1, 128))
    got = lax.all_to_all(jnp.concatenate(flat, axis=1), axis, 0, 0, tiled=True)
    out, start = [], 0
    for p, f in zip(parts, flat):
        piece = got[:, start : start + f.shape[1]].reshape(count, -1)
        out.append(piece[:, : p[0].size].reshape(p.shape))
        start += f.shape[1]
    return out


def to_all(value, count):
    return jnp.broadcast_to(value[None], (count,) + value.shape)


def split_wide(value):
    high = lax.reduce_precision(value, exponent_bits=8, mantissa_bits=7)
    return jnp.concatenate([high, value - high], axis=-1).astype(BF16)


def join_wide(value):
    half = value.shape[-1] // 2
    wide = value.astype(F32)
    return wide[..., :half] + wide[..., half:]


def shards(features, conv_weight, down_weight, cotangent, partner, orientation):
    tiles, share, _ = features.shape
    n_chan = lax.axis_size("chan")
    n_space = lax.axis_size("space")
    in_channels = share * n_chan
    out_share = conv_weight.shape[0]
    out_channels = out_share * n_chan
    rows = S // n_chan
    half = S // 2
    conv_cols = conv_weight.shape[1] * conv_weight.shape[2]
    down_cols = down_weight.shape[1] * down_weight.shape[2]

    weights = jnp.concatenate(
        [conv_weight.reshape(out_share, conv_cols), down_weight.reshape(out_share, down_cols)], axis=1
    )

    images = features.reshape(tiles, share, S, S)
    flat_in = features
    strips = jnp.stack(
        [flat_in[..., :S], flat_in[..., S - 1 :: S], flat_in[..., S * (S - 1) :], flat_in[..., ::S]], axis=1
    )
    (strips_all,) = exchange([to_all(strips, n_space)], "space")
    halo = bordering(strips_all.reshape((n_space * tiles,) + strips.shape[1:]), partner, orientation)
    padded = pad_cat(images, halo)

    head = padded[:, :, : S, :].reshape(tiles, share, n_chan, rows, S + 2)
    tail = jnp.pad(padded[:, :, rows:, :], ((0, 0), (0, 0), (0, rows - 2), (0, 0)))
    tail = tail.reshape(tiles, share, n_chan, rows, S + 2)[:, :, :, :2, :]
    bands = jnp.moveaxis(jnp.concatenate([head, tail], axis=3), 2, 0)
    cot_bands = jnp.moveaxis(cotangent.reshape(tiles, out_share, n_chan, rows // 2 * half), 2, 0)
    cot_in, w_in, band_in = exchange([cot_bands, to_all(weights, n_chan), bands], "chan")
    block = jnp.moveaxis(band_in, 0, 1).reshape(tiles, in_channels, rows + 2, S + 2)
    grad_band = jnp.moveaxis(cot_in, 0, 1).reshape(tiles, out_channels, rows // 2, half)
    w_full = w_in.reshape(out_channels, conv_cols + down_cols)
    conv_full = w_full[:, :conv_cols].reshape(out_channels, 9, in_channels)
    down_full = w_full[:, conv_cols:].reshape(out_channels, 4, out_channels)

    plain = ("NCHW", "OIHW", "NCHW")
    swapped = ("CNHW", "IOHW", "NCHW")
    w_conv = conv_full.reshape(out_channels, 3, 3, in_channels).transpose(0, 3, 1, 2)
    w_down = down_full.reshape(out_channels, 2, 2, out_channels).transpose(0, 3, 1, 2)
    pre_act = lax.conv_general_dilated(
        block, w_conv, (1, 1), "VALID", dimension_numbers=plain, preferred_element_type=F32
    )
    activated = jax.nn.silu(pre_act).astype(BF16)
    pooled_rows = lax.conv_general_dilated(
        activated, w_down, (2, 2), "VALID", dimension_numbers=plain, preferred_element_type=F32
    ).astype(BF16)
    down_part = lax.conv_general_dilated(
        activated, grad_band, (1, 1), "VALID", rhs_dilation=(2, 2),
        dimension_numbers=swapped, preferred_element_type=F32,
    )
    down_part = down_part.transpose(1, 2, 3, 0).reshape(out_channels, down_cols)
    w_up = jnp.flip(w_down, (2, 3)).transpose(1, 0, 2, 3)
    grad_act = lax.conv_general_dilated(
        grad_band, w_up, (1, 1), ((1, 1), (1, 1)), lhs_dilation=(2, 2),
        dimension_numbers=plain, preferred_element_type=F32,
    )
    grad_pre = (grad_act * silu_grad(pre_act)).astype(BF16)
    conv_part = lax.conv_general_dilated(
        block, grad_pre, (1, 1), "VALID", dimension_numbers=swapped, preferred_element_type=F32
    )
    conv_part = conv_part.transpose(1, 2, 3, 0).reshape(out_channels, conv_cols)
    w_back_conv = jnp.flip(w_conv, (2, 3)).transpose(1, 0, 2, 3)
    grad_block = lax.conv_general_dilated(
        grad_pre, w_back_conv, (1, 1), ((2, 2), (2, 2)), dimension_numbers=plain,
        preferred_element_type=F32,
    )

    pooled_out = jnp.moveaxis(pooled_rows.reshape(tiles, n_chan, out_share, rows // 2 * half), 1, 0)
    grad_out = jnp.moveaxis(
        grad_block.astype(BF16).reshape(tiles, n_chan, share, rows + 2, S + 2), 1, 0
    )
    down_dest = down_part.reshape(n_chan, out_share * down_cols)
    conv_dest = conv_part.reshape(n_chan, out_share, 9, in_channels).transpose(0, 2, 1, 3)
    w_part = jnp.concatenate([down_dest, conv_dest.reshape(n_chan, out_share * conv_cols)], axis=1)
    w_part = split_wide(w_part)
    pooled_in, w_back, grad_in = exchange([pooled_out, w_part, grad_out], "chan")
    pooled = jnp.moveaxis(pooled_in, 0, 2).reshape(tiles, out_share, half * half)
    w_sum = jnp.sum(join_wide(w_back), axis=0)

    g = grad_in.astype(F32)
    main = jnp.moveaxis(g[:, :, :, :rows, :], 0, 2).reshape(tiles, share, S, S + 2)
    extra = jnp.pad(g[:, :, :, rows:, :], ((0, 0), (0, 0), (0, 0), (0, rows - 2), (0, 0)))
    extra = jnp.moveaxis(extra, 0, 2).reshape(tiles, share, S, S + 2)
    grad_padded = jnp.pad(main, ((0, 0), (0, 0), (0, 2), (0, 0))) + jnp.pad(
        extra, ((0, 0), (0, 0), (rows, 0), (0, 0))
    )[:, :, : S + 2, :]

    rims = rim_strips(grad_padded)
    w_len = w_sum.shape[0]
    piece = -(-w_len // n_space)
    w_pieces = jnp.pad(w_sum, (0, piece * n_space - w_len)).reshape(n_space, piece)
    rims_all, w_got = exchange([to_all(rims.astype(BF16), n_space), split_wide(w_pieces)], "space")
    grad_scale = float(n_space * tiles * S * S) ** (-0.5)
    w_mine = jnp.sum(join_wide(w_got), axis=0) * grad_scale
    (w_all,) = exchange([to_all(w_mine, n_space)], "space")
    w_total = w_all.reshape(-1)[:w_len]

    returned = bordering(rims_all.reshape((n_space * tiles,) + rims.shape[1:]), partner, orientation)
    returned = returned.astype(F32)
    features_grad = add_edges(grad_padded[:, :, 1:-1, 1:-1], returned).astype(BF16)
    features_grad = features_grad.reshape(tiles, share, S * S)
    down_len = out_share * down_cols
    down_grad = w_total[:down_len].reshape(down_weight.shape)
    conv_grad = w_total[down_len:].reshape(9, out_share, in_channels).transpose(1, 0, 2)
    return (pooled, features_grad, conv_grad, down_grad)


def solution(mesh):
    placed = (
        P("space", "chan", None),
        P("chan", None, None),
        P("chan", None, None),
        P("space", "chan", None),
        P("space", None),
        P("space", None),
    )
    return jax.shard_map(
        shards,
        mesh=mesh,
        in_specs=placed,
        out_specs=(
            P("space", "chan", None),
            P("space", "chan", None),
            P("chan", None, None),
            P("chan", None, None),
        ),
        check_vma=False,
    )
```

```python
import jax
import jax.numpy as jnp
from jax import lax
from jax.sharding import PartitionSpec as P

S = 64
F32 = jnp.float32
BF16 = jnp.bfloat16


def edge_strips(values):
    return jnp.stack(
        [values[..., 0, :], values[..., :, -1], values[..., -1, :], values[..., :, 0]], axis=-3
    )


def rim_strips(padded):
    return jnp.stack(
        [padded[..., 0, 1:-1], padded[..., 1:-1, -1], padded[..., -1, 1:-1], padded[..., 1:-1, 0]],
        axis=-3,
    )


def bordering(strips, partner, orientation):
    flat = strips.reshape((-1,) + strips.shape[2:])
    picked = jnp.take(flat, partner.reshape(-1), axis=0)
    picked = picked.reshape(partner.shape + strips.shape[2:])
    return jnp.where((orientation == 1)[..., None, None], picked[..., ::-1], picked)


def pad_tile(values, halo_strips):
    tile_side = values.shape[-1]
    widths = [(0, 0)] * (values.ndim - 2) + [(1, 1), (1, 1)]
    padded = jnp.pad(values, widths)
    padded = padded.at[..., 0, 1 : tile_side + 1].set(halo_strips[..., 0, :, :])
    padded = padded.at[..., 1 : tile_side + 1, tile_side + 1].set(halo_strips[..., 1, :, :])
    padded = padded.at[..., tile_side + 1, 1 : tile_side + 1].set(halo_strips[..., 2, :, :])
    return padded.at[..., 1 : tile_side + 1, 0].set(halo_strips[..., 3, :, :])


def pad_cat(values, halo):
    zero = jnp.zeros(values.shape[:2] + (1, 1), values.dtype)
    top = jnp.concatenate([zero, halo[:, 0, :, None, :], zero], axis=3)
    bottom = jnp.concatenate([zero, halo[:, 2, :, None, :], zero], axis=3)
    middle = jnp.concatenate([halo[:, 3, :, :, None], values, halo[:, 1, :, :, None]], axis=3)
    return jnp.concatenate([top, middle, bottom], axis=2)


def add_edges(interior, returned):
    n = interior.shape[-1]
    none = ((0, 0), (0, 0))
    rows = jnp.pad(returned[:, 0, :, None, :], none + ((0, n - 1), (0, 0))) + jnp.pad(
        returned[:, 2, :, None, :], none + ((n - 1, 0), (0, 0))
    )
    cols = jnp.pad(returned[:, 3, :, :, None], none + ((0, 0), (0, n - 1))) + jnp.pad(
        returned[:, 1, :, :, None], none + ((0, 0), (n - 1, 0))
    )
    return interior + (rows + cols)


def unfold(padded, height, width):
    taps = [
        padded[..., row_shift : row_shift + height, col_shift : col_shift + width]
        for row_shift in range(3)
        for col_shift in range(3)
    ]
    return jnp.stack(taps, axis=-4)


def fold_taps(taps):
    total = None
    for row_shift in range(3):
        for col_shift in range(3):
            piece = taps[..., 3 * row_shift + col_shift, :, :, :]
            widths = [(0, 0)] * (piece.ndim - 2) + [
                (row_shift, 2 - row_shift),
                (col_shift, 2 - col_shift),
            ]
            placed = jnp.pad(piece, widths)
            total = placed if total is None else total + placed
    return total


def silu_grad(values):
    gate = jax.nn.sigmoid(values)
    return gate * (1.0 + values * (1.0 - gate))


def exchange(parts, axis):
    count = parts[0].shape[0]
    tile = 4096 // parts[0].dtype.itemsize
    flat = []
    for i, p in enumerate(parts):
        size = p[0].size
        step = 128 if i == len(parts) - 1 else tile
        padded = jnp.pad(p.reshape(count, size), ((0, 0), (0, -size % step)))
        flat.append(padded.reshape(count, -1, 128))
    got = lax.all_to_all(jnp.concatenate(flat, axis=1), axis, 0, 0, tiled=True)
    out, start = [], 0
    for p, f in zip(parts, flat):
        piece = got[:, start : start + f.shape[1]].reshape(count, -1)
        out.append(piece[:, : p[0].size].reshape(p.shape))
        start += f.shape[1]
    return out


def to_all(value, count):
    return jnp.broadcast_to(value[None], (count,) + value.shape)


def split_wide(value):
    high = lax.reduce_precision(value, exponent_bits=8, mantissa_bits=7)
    return jnp.concatenate([high, value - high], axis=-1).astype(BF16)


def join_wide(value):
    half = value.shape[-1] // 2
    wide = value.astype(F32)
    return wide[..., :half] + wide[..., half:]


def shards(features, conv_weight, down_weight, cotangent, partner, orientation):
    tiles, share, _ = features.shape
    n_chan = lax.axis_size("chan")
    n_space = lax.axis_size("space")
    in_channels = share * n_chan
    out_share = conv_weight.shape[0]
    out_channels = out_share * n_chan
    rows = S // n_chan
    half = S // 2
    conv_cols = conv_weight.shape[1] * conv_weight.shape[2]
    down_cols = down_weight.shape[1] * down_weight.shape[2]

    weights = jnp.concatenate(
        [conv_weight.reshape(out_share, conv_cols), down_weight.reshape(out_share, down_cols)], axis=1
    )

    images = features.reshape(tiles, share, S, S)
    strips = edge_strips(images)
    (strips_all,) = exchange([to_all(strips, n_space)], "space")
    halo = bordering(strips_all.reshape((n_space * tiles,) + strips.shape[1:]), partner, orientation)
    padded = pad_cat(images, halo)

    head = padded[:, :, : S, :].reshape(tiles, share, n_chan, rows, S + 2)
    tail = jnp.pad(padded[:, :, rows:, :], ((0, 0), (0, 0), (0, rows - 2), (0, 0)))
    tail = tail.reshape(tiles, share, n_chan, rows, S + 2)[:, :, :, :2, :]
    bands = jnp.moveaxis(jnp.concatenate([head, tail], axis=3), 2, 0)
    cot_bands = jnp.moveaxis(cotangent.reshape(tiles, out_share, n_chan, rows // 2 * half), 2, 0)
    cot_in, w_in, band_in = exchange([cot_bands, to_all(weights, n_chan), bands], "chan")
    block = jnp.moveaxis(band_in, 0, 1).reshape(tiles, in_channels, rows + 2, S + 2)
    grad_band = jnp.moveaxis(cot_in, 0, 1).reshape(tiles, out_channels, rows // 2, half)
    w_full = w_in.reshape(out_channels, conv_cols + down_cols)
    conv_full = w_full[:, :conv_cols].reshape(out_channels, 9, in_channels)
    down_full = w_full[:, conv_cols:].reshape(out_channels, 4, out_channels)

    plain = ("NCHW", "OIHW", "NCHW")
    swapped = ("CNHW", "IOHW", "NCHW")
    w_conv = conv_full.reshape(out_channels, 3, 3, in_channels).transpose(0, 3, 1, 2)
    w_down = down_full.reshape(out_channels, 2, 2, out_channels).transpose(0, 3, 1, 2)
    pre_act = lax.conv_general_dilated(
        block, w_conv, (1, 1), "VALID", dimension_numbers=plain, preferred_element_type=F32
    )
    activated = jax.nn.silu(pre_act).astype(BF16)
    pooled_rows = lax.conv_general_dilated(
        activated, w_down, (2, 2), "VALID", dimension_numbers=plain, preferred_element_type=F32
    ).astype(BF16)
    down_part = lax.conv_general_dilated(
        activated, grad_band, (1, 1), "VALID", rhs_dilation=(2, 2),
        dimension_numbers=swapped, preferred_element_type=F32,
    )
    down_part = down_part.transpose(1, 2, 3, 0).reshape(out_channels, down_cols)
    w_up = jnp.flip(w_down, (2, 3)).transpose(1, 0, 2, 3)
    grad_act = lax.conv_general_dilated(
        grad_band, w_up, (1, 1), ((1, 1), (1, 1)), lhs_dilation=(2, 2),
        dimension_numbers=plain, preferred_element_type=F32,
    )
    grad_pre = (grad_act * silu_grad(pre_act)).astype(BF16)
    conv_part = lax.conv_general_dilated(
        block, grad_pre, (1, 1), "VALID", dimension_numbers=swapped, preferred_element_type=F32
    )
    conv_part = conv_part.transpose(1, 2, 3, 0).reshape(out_channels, conv_cols)
    w_back_conv = jnp.flip(w_conv, (2, 3)).transpose(1, 0, 2, 3)
    grad_block = lax.conv_general_dilated(
        grad_pre, w_back_conv, (1, 1), ((2, 2), (2, 2)), dimension_numbers=plain,
        preferred_element_type=F32,
    )

    pooled_out = jnp.moveaxis(pooled_rows.reshape(tiles, n_chan, out_share, rows // 2 * half), 1, 0)
    grad_out = jnp.moveaxis(
        grad_block.astype(BF16).reshape(tiles, n_chan, share, rows + 2, S + 2), 1, 0
    )
    down_dest = down_part.reshape(n_chan, out_share * down_cols)
    conv_dest = conv_part.reshape(n_chan, out_share, 9, in_channels).transpose(0, 2, 1, 3)
    w_part = jnp.concatenate([down_dest, conv_dest.reshape(n_chan, out_share * conv_cols)], axis=1)
    w_part = split_wide(w_part)
    pooled_in, w_back, grad_in = exchange([pooled_out, w_part, grad_out], "chan")
    pooled = jnp.moveaxis(pooled_in, 0, 2).reshape(tiles, out_share, half * half)
    w_sum = jnp.sum(join_wide(w_back), axis=0)

    g = grad_in.astype(F32)
    main = jnp.moveaxis(g[:, :, :, :rows, :], 0, 2).reshape(tiles, share, S, S + 2)
    extra = jnp.pad(g[:, :, :, rows:, :], ((0, 0), (0, 0), (0, 0), (0, rows - 2), (0, 0)))
    extra = jnp.moveaxis(extra, 0, 2).reshape(tiles, share, S, S + 2)
    grad_padded = jnp.pad(main, ((0, 0), (0, 0), (0, 2), (0, 0))) + jnp.pad(
        extra, ((0, 0), (0, 0), (rows, 0), (0, 0))
    )[:, :, : S + 2, :]

    rims = rim_strips(grad_padded)
    w_len = w_sum.shape[0]
    piece = -(-w_len // (n_space * 128)) * 128
    w_pieces = jnp.pad(w_sum, (0, piece * n_space - w_len)).reshape(n_space, piece)
    rims_all, w_got = exchange([to_all(rims.astype(BF16), n_space), split_wide(w_pieces)], "space")
    grad_scale = float(n_space * tiles * S * S) ** (-0.5)
    w_mine = jnp.sum(join_wide(w_got), axis=0) * grad_scale
    (w_all,) = exchange([to_all(w_mine, n_space)], "space")
    w_total = w_all.reshape(-1)[:w_len]

    returned = bordering(rims_all.reshape((n_space * tiles,) + rims.shape[1:]), partner, orientation)
    returned = returned.astype(F32)
    features_grad = add_edges(grad_padded[:, :, 1:-1, 1:-1], returned).astype(BF16)
    features_grad = features_grad.reshape(tiles, share, S * S)
    down_len = out_share * down_cols
    down_grad = w_total[:down_len].reshape(down_weight.shape)
    conv_grad = w_total[down_len:].reshape(9, out_share, in_channels).transpose(1, 0, 2)
    return (pooled, features_grad, conv_grad, down_grad)


def solution(mesh):
    placed = (
        P("space", "chan", None),
        P("chan", None, None),
        P("chan", None, None),
        P("space", "chan", None),
        P("space", None),
        P("space", None),
    )
    return jax.shard_map(
        shards,
        mesh=mesh,
        in_specs=placed,
        out_specs=(
            P("space", "chan", None),
            P("space", "chan", None),
            P("chan", None, None),
            P("chan", None, None),
        ),
        check_vma=False,
    )
```

```python
import jax
import jax.numpy as jnp
from jax import lax
from jax.sharding import PartitionSpec as P

S = 64
F32 = jnp.float32
BF16 = jnp.bfloat16


def edge_strips(values):
    return jnp.stack(
        [values[..., 0, :], values[..., :, -1], values[..., -1, :], values[..., :, 0]], axis=-3
    )


def rim_strips(padded):
    return jnp.stack(
        [padded[..., 0, 1:-1], padded[..., 1:-1, -1], padded[..., -1, 1:-1], padded[..., 1:-1, 0]],
        axis=-3,
    )


def bordering(strips, partner, orientation):
    flat = strips.reshape((-1,) + strips.shape[2:])
    picked = jnp.take(flat, partner.reshape(-1), axis=0)
    picked = picked.reshape(partner.shape + strips.shape[2:])
    return jnp.where((orientation == 1)[..., None, None], picked[..., ::-1], picked)


def pad_tile(values, halo_strips):
    tile_side = values.shape[-1]
    widths = [(0, 0)] * (values.ndim - 2) + [(1, 1), (1, 1)]
    padded = jnp.pad(values, widths)
    padded = padded.at[..., 0, 1 : tile_side + 1].set(halo_strips[..., 0, :, :])
    padded = padded.at[..., 1 : tile_side + 1, tile_side + 1].set(halo_strips[..., 1, :, :])
    padded = padded.at[..., tile_side + 1, 1 : tile_side + 1].set(halo_strips[..., 2, :, :])
    return padded.at[..., 1 : tile_side + 1, 0].set(halo_strips[..., 3, :, :])


def pad_cat(values, halo):
    zero = jnp.zeros(values.shape[:2] + (1, 1), values.dtype)
    top = jnp.concatenate([zero, halo[:, 0, :, None, :], zero], axis=3)
    bottom = jnp.concatenate([zero, halo[:, 2, :, None, :], zero], axis=3)
    middle = jnp.concatenate([halo[:, 3, :, :, None], values, halo[:, 1, :, :, None]], axis=3)
    return jnp.concatenate([top, middle, bottom], axis=2)


def add_edges(interior, returned):
    n = interior.shape[-1]
    none = ((0, 0), (0, 0))
    rows = jnp.pad(returned[:, 0, :, None, :], none + ((0, n - 1), (0, 0))) + jnp.pad(
        returned[:, 2, :, None, :], none + ((n - 1, 0), (0, 0))
    )
    cols = jnp.pad(returned[:, 3, :, :, None], none + ((0, 0), (0, n - 1))) + jnp.pad(
        returned[:, 1, :, :, None], none + ((0, 0), (n - 1, 0))
    )
    return interior + (rows + cols)


def unfold(padded, height, width):
    taps = [
        padded[..., row_shift : row_shift + height, col_shift : col_shift + width]
        for row_shift in range(3)
        for col_shift in range(3)
    ]
    return jnp.stack(taps, axis=-4)


def fold_taps(taps):
    total = None
    for row_shift in range(3):
        for col_shift in range(3):
            piece = taps[..., 3 * row_shift + col_shift, :, :, :]
            widths = [(0, 0)] * (piece.ndim - 2) + [
                (row_shift, 2 - row_shift),
                (col_shift, 2 - col_shift),
            ]
            placed = jnp.pad(piece, widths)
            total = placed if total is None else total + placed
    return total


def silu_grad(values):
    gate = jax.nn.sigmoid(values)
    return gate * (1.0 + values * (1.0 - gate))


def exchange(parts, axis):
    count = parts[0].shape[0]
    tile = 4096 // parts[0].dtype.itemsize
    flat = []
    for i, p in enumerate(parts):
        size = p[0].size
        step = 128 if i == len(parts) - 1 else tile
        padded = jnp.pad(p.reshape(count, size), ((0, 0), (0, -size % step)))
        flat.append(padded.reshape(count, -1, 128))
    got = lax.all_to_all(jnp.concatenate(flat, axis=1), axis, 0, 0, tiled=True)
    out, start = [], 0
    for p, f in zip(parts, flat):
        piece = got[:, start : start + f.shape[1]].reshape(count, -1)
        out.append(piece[:, : p[0].size].reshape(p.shape))
        start += f.shape[1]
    return out


def to_all(value, count):
    return jnp.broadcast_to(value[None], (count,) + value.shape)


def split_wide(value):
    high = lax.reduce_precision(value, exponent_bits=8, mantissa_bits=7)
    return jnp.concatenate([high, value - high], axis=-1).astype(BF16)


def join_wide(value):
    half = value.shape[-1] // 2
    wide = value.astype(F32)
    return wide[..., :half] + wide[..., half:]


def shards(features, conv_weight, down_weight, cotangent, partner, orientation):
    tiles, share, _ = features.shape
    n_chan = lax.axis_size("chan")
    n_space = lax.axis_size("space")
    in_channels = share * n_chan
    out_share = conv_weight.shape[0]
    out_channels = out_share * n_chan
    rows = S // n_chan
    half = S // 2
    conv_cols = conv_weight.shape[1] * conv_weight.shape[2]
    down_cols = down_weight.shape[1] * down_weight.shape[2]

    weights = jnp.concatenate(
        [conv_weight.reshape(out_share, conv_cols), down_weight.reshape(out_share, down_cols)], axis=1
    )

    images = features.reshape(tiles, share, S, S)
    strips = edge_strips(images)
    (strips_all,) = exchange([to_all(strips, n_space)], "space")
    halo = bordering(strips_all.reshape((n_space * tiles,) + strips.shape[1:]), partner, orientation)
    padded = pad_cat(images, halo)

    head = padded[:, :, : S, :].reshape(tiles, share, n_chan, rows, S + 2)
    tail = jnp.pad(padded[:, :, rows:, :], ((0, 0), (0, 0), (0, rows - 2), (0, 0)))
    tail = tail.reshape(tiles, share, n_chan, rows, S + 2)[:, :, :, :2, :]
    bands = jnp.moveaxis(jnp.concatenate([head, tail], axis=3), 2, 0)
    cot_bands = jnp.moveaxis(cotangent.reshape(tiles, out_share, n_chan, rows // 2 * half), 2, 0)
    cot_in, w_in, band_in = exchange([cot_bands, to_all(weights, n_chan), bands], "chan")
    block = jnp.moveaxis(band_in, 0, 1).reshape(tiles, in_channels, rows + 2, S + 2)
    grad_band = jnp.moveaxis(cot_in, 0, 1).reshape(tiles, out_channels, rows // 2, half)
    w_full = w_in.reshape(out_channels, conv_cols + down_cols)
    conv_full = w_full[:, :conv_cols].reshape(out_channels, 9, in_channels)
    down_full = w_full[:, conv_cols:].reshape(out_channels, 4, out_channels)

    plain = ("NCHW", "OIHW", "NCHW")
    swapped = ("CNHW", "IOHW", "NCHW")
    w_conv = conv_full.reshape(out_channels, 3, 3, in_channels).transpose(0, 3, 1, 2)
    w_down = down_full.reshape(out_channels, 2, 2, out_channels).transpose(0, 3, 1, 2)
    pre_act = lax.conv_general_dilated(
        block, w_conv, (1, 1), "VALID", dimension_numbers=plain, preferred_element_type=F32
    )
    activated = jax.nn.silu(pre_act).astype(BF16)
    pooled_rows = lax.conv_general_dilated(
        activated, w_down, (2, 2), "VALID", dimension_numbers=plain, preferred_element_type=F32
    ).astype(BF16)
    down_part = lax.conv_general_dilated(
        activated, grad_band, (1, 1), "VALID", rhs_dilation=(2, 2),
        dimension_numbers=swapped, preferred_element_type=F32,
    )
    down_part = down_part.transpose(1, 2, 3, 0).reshape(out_channels, down_cols)
    w_up = jnp.flip(w_down, (2, 3)).transpose(1, 0, 2, 3)
    grad_act = lax.conv_general_dilated(
        grad_band, w_up, (1, 1), ((1, 1), (1, 1)), lhs_dilation=(2, 2),
        dimension_numbers=plain, preferred_element_type=F32,
    )
    grad_pre = (grad_act * silu_grad(pre_act)).astype(BF16)
    conv_part = lax.conv_general_dilated(
        block, grad_pre, (1, 1), "VALID", dimension_numbers=swapped, preferred_element_type=F32
    )
    conv_part = conv_part.transpose(1, 2, 3, 0).reshape(out_channels, conv_cols)
    _, data_grad = jax.vjp(
        lambda x: lax.conv_general_dilated(x, w_conv, (1, 1), "VALID", dimension_numbers=plain), block
    )
    (grad_block,) = data_grad(grad_pre)

    pooled_out = jnp.moveaxis(pooled_rows.reshape(tiles, n_chan, out_share, rows // 2 * half), 1, 0)
    grad_out = jnp.moveaxis(
        grad_block.astype(BF16).reshape(tiles, n_chan, share, rows + 2, S + 2), 1, 0
    )
    down_dest = down_part.reshape(n_chan, out_share * down_cols)
    conv_dest = conv_part.reshape(n_chan, out_share, 9, in_channels).transpose(0, 2, 1, 3)
    w_part = jnp.concatenate([down_dest, conv_dest.reshape(n_chan, out_share * conv_cols)], axis=1)
    w_part = split_wide(w_part)
    pooled_in, w_back, grad_in = exchange([pooled_out, w_part, grad_out], "chan")
    pooled = jnp.moveaxis(pooled_in, 0, 2).reshape(tiles, out_share, half * half)
    w_sum = jnp.sum(join_wide(w_back), axis=0)

    g = grad_in.astype(F32)
    main = jnp.moveaxis(g[:, :, :, :rows, :], 0, 2).reshape(tiles, share, S, S + 2)
    extra = jnp.pad(g[:, :, :, rows:, :], ((0, 0), (0, 0), (0, 0), (0, rows - 2), (0, 0)))
    extra = jnp.moveaxis(extra, 0, 2).reshape(tiles, share, S, S + 2)
    grad_padded = jnp.pad(main, ((0, 0), (0, 0), (0, 2), (0, 0))) + jnp.pad(
        extra, ((0, 0), (0, 0), (rows, 0), (0, 0))
    )[:, :, : S + 2, :]

    rims = rim_strips(grad_padded)
    w_len = w_sum.shape[0]
    piece = -(-w_len // (n_space * 128)) * 128
    w_pieces = jnp.pad(w_sum, (0, piece * n_space - w_len)).reshape(n_space, piece)
    rims_all, w_got = exchange([to_all(rims.astype(BF16), n_space), split_wide(w_pieces)], "space")
    grad_scale = float(n_space * tiles * S * S) ** (-0.5)
    w_mine = jnp.sum(join_wide(w_got), axis=0) * grad_scale
    (w_all,) = exchange([to_all(w_mine, n_space)], "space")
    w_total = w_all.reshape(-1)[:w_len]

    returned = bordering(rims_all.reshape((n_space * tiles,) + rims.shape[1:]), partner, orientation)
    returned = returned.astype(F32)
    features_grad = add_edges(grad_padded[:, :, 1:-1, 1:-1], returned).astype(BF16)
    features_grad = features_grad.reshape(tiles, share, S * S)
    down_len = out_share * down_cols
    down_grad = w_total[:down_len].reshape(down_weight.shape)
    conv_grad = w_total[down_len:].reshape(9, out_share, in_channels).transpose(1, 0, 2)
    return (pooled, features_grad, conv_grad, down_grad)


def solution(mesh):
    placed = (
        P("space", "chan", None),
        P("chan", None, None),
        P("chan", None, None),
        P("space", "chan", None),
        P("space", None),
        P("space", None),
    )
    return jax.shard_map(
        shards,
        mesh=mesh,
        in_specs=placed,
        out_specs=(
            P("space", "chan", None),
            P("space", "chan", None),
            P("chan", None, None),
            P("chan", None, None),
        ),
        check_vma=False,
    )
```

```python
import jax
import jax.numpy as jnp
from jax import lax
from jax.sharding import PartitionSpec as P

S = 64
F32 = jnp.float32
BF16 = jnp.bfloat16


def edge_strips(values):
    return jnp.stack(
        [values[..., 0, :], values[..., :, -1], values[..., -1, :], values[..., :, 0]], axis=-3
    )


def rim_strips(padded):
    return jnp.stack(
        [padded[..., 0, 1:-1], padded[..., 1:-1, -1], padded[..., -1, 1:-1], padded[..., 1:-1, 0]],
        axis=-3,
    )


def bordering(strips, partner, orientation):
    flat = strips.reshape((-1,) + strips.shape[2:])
    picked = jnp.take(flat, partner.reshape(-1), axis=0)
    picked = picked.reshape(partner.shape + strips.shape[2:])
    return jnp.where((orientation == 1)[..., None, None], picked[..., ::-1], picked)


def pad_tile(values, halo_strips):
    tile_side = values.shape[-1]
    widths = [(0, 0)] * (values.ndim - 2) + [(1, 1), (1, 1)]
    padded = jnp.pad(values, widths)
    padded = padded.at[..., 0, 1 : tile_side + 1].set(halo_strips[..., 0, :, :])
    padded = padded.at[..., 1 : tile_side + 1, tile_side + 1].set(halo_strips[..., 1, :, :])
    padded = padded.at[..., tile_side + 1, 1 : tile_side + 1].set(halo_strips[..., 2, :, :])
    return padded.at[..., 1 : tile_side + 1, 0].set(halo_strips[..., 3, :, :])


def pad_cat(values, halo):
    zero = jnp.zeros(values.shape[:2] + (1, 1), values.dtype)
    top = jnp.concatenate([zero, halo[:, 0, :, None, :], zero], axis=3)
    bottom = jnp.concatenate([zero, halo[:, 2, :, None, :], zero], axis=3)
    middle = jnp.concatenate([halo[:, 3, :, :, None], values, halo[:, 1, :, :, None]], axis=3)
    return jnp.concatenate([top, middle, bottom], axis=2)


def add_edges(interior, returned):
    n = interior.shape[-1]
    none = ((0, 0), (0, 0))
    rows = jnp.pad(returned[:, 0, :, None, :], none + ((0, n - 1), (0, 0))) + jnp.pad(
        returned[:, 2, :, None, :], none + ((n - 1, 0), (0, 0))
    )
    cols = jnp.pad(returned[:, 3, :, :, None], none + ((0, 0), (0, n - 1))) + jnp.pad(
        returned[:, 1, :, :, None], none + ((0, 0), (n - 1, 0))
    )
    return interior + (rows + cols)


def unfold(padded, height, width):
    taps = [
        padded[..., row_shift : row_shift + height, col_shift : col_shift + width]
        for row_shift in range(3)
        for col_shift in range(3)
    ]
    return jnp.stack(taps, axis=-4)


def fold_taps(taps):
    total = None
    for row_shift in range(3):
        for col_shift in range(3):
            piece = taps[..., 3 * row_shift + col_shift, :, :, :]
            widths = [(0, 0)] * (piece.ndim - 2) + [
                (row_shift, 2 - row_shift),
                (col_shift, 2 - col_shift),
            ]
            placed = jnp.pad(piece, widths)
            total = placed if total is None else total + placed
    return total


def silu_grad(values):
    gate = jax.nn.sigmoid(values)
    return gate * (1.0 + values * (1.0 - gate))


def exchange(parts, axis):
    count = parts[0].shape[0]
    tile = 4096 // parts[0].dtype.itemsize
    flat = []
    for i, p in enumerate(parts):
        size = p[0].size
        step = 128 if i == len(parts) - 1 else tile
        padded = jnp.pad(p.reshape(count, size), ((0, 0), (0, -size % step)))
        flat.append(padded.reshape(count, -1, 128))
    got = lax.all_to_all(jnp.concatenate(flat, axis=1), axis, 0, 0, tiled=True)
    out, start = [], 0
    for p, f in zip(parts, flat):
        piece = got[:, start : start + f.shape[1]].reshape(count, -1)
        out.append(piece[:, : p[0].size].reshape(p.shape))
        start += f.shape[1]
    return out


def to_all(value, count):
    return jnp.broadcast_to(value[None], (count,) + value.shape)


def split_wide(value):
    high = lax.reduce_precision(value, exponent_bits=8, mantissa_bits=7)
    return jnp.concatenate([high, value - high], axis=-1).astype(BF16)


def join_wide(value):
    half = value.shape[-1] // 2
    wide = value.astype(F32)
    return wide[..., :half] + wide[..., half:]


def shards(features, conv_weight, down_weight, cotangent, partner, orientation):
    tiles, share, _ = features.shape
    n_chan = lax.axis_size("chan")
    n_space = lax.axis_size("space")
    in_channels = share * n_chan
    out_share = conv_weight.shape[0]
    out_channels = out_share * n_chan
    rows = S // n_chan
    half = S // 2
    conv_cols = conv_weight.shape[1] * conv_weight.shape[2]
    down_cols = down_weight.shape[1] * down_weight.shape[2]

    weights = jnp.concatenate(
        [conv_weight.reshape(out_share, conv_cols), down_weight.reshape(out_share, down_cols)], axis=1
    )

    images = features.reshape(tiles, share, S, S)
    strips = edge_strips(images)
    (strips_all,) = exchange([to_all(strips, n_space)], "space")
    halo = bordering(strips_all.reshape((n_space * tiles,) + strips.shape[1:]), partner, orientation)
    padded = pad_cat(images, halo)

    head = padded[:, :, : S, :].reshape(tiles, share, n_chan, rows, S + 2)
    tail = jnp.pad(padded[:, :, rows:, :], ((0, 0), (0, 0), (0, rows - 2), (0, 0)))
    tail = tail.reshape(tiles, share, n_chan, rows, S + 2)[:, :, :, :2, :]
    bands = jnp.moveaxis(jnp.concatenate([head, tail], axis=3), 2, 0)
    cot_bands = jnp.moveaxis(cotangent.reshape(tiles, out_share, n_chan, rows // 2 * half), 2, 0)
    cot_in, w_in, band_in = exchange([cot_bands, to_all(weights, n_chan), bands], "chan")
    block = jnp.moveaxis(band_in, 0, 1).reshape(tiles, in_channels, rows + 2, S + 2)
    grad_band = jnp.moveaxis(cot_in, 0, 1).reshape(tiles, out_channels, rows // 2, half)
    w_full = w_in.reshape(out_channels, conv_cols + down_cols)
    conv_full = w_full[:, :conv_cols].reshape(out_channels, 9, in_channels)
    down_full = w_full[:, conv_cols:].reshape(out_channels, 4, out_channels)

    plain = ("NCHW", "OIHW", "NCHW")
    swapped = ("CNHW", "IOHW", "NCHW")
    w_conv = conv_full.reshape(out_channels, 3, 3, in_channels).transpose(0, 3, 1, 2)
    w_down = down_full.reshape(out_channels, 2, 2, out_channels).transpose(0, 3, 1, 2)
    pre_act = lax.conv_general_dilated(
        block, w_conv, (1, 1), "VALID", dimension_numbers=plain, preferred_element_type=F32
    )
    activated = jax.nn.silu(pre_act).astype(BF16)
    pooled_rows = lax.conv_general_dilated(
        activated, w_down, (2, 2), "VALID", dimension_numbers=plain, preferred_element_type=F32
    ).astype(BF16)
    down_part = lax.conv_general_dilated(
        activated, grad_band, (1, 1), "VALID", rhs_dilation=(2, 2),
        dimension_numbers=swapped, preferred_element_type=F32,
    )
    down_part = down_part.transpose(1, 2, 3, 0).reshape(out_channels, down_cols)
    w_up = jnp.flip(w_down, (2, 3)).transpose(1, 0, 2, 3)
    grad_act = lax.conv_general_dilated(
        grad_band, w_up, (1, 1), ((1, 1), (1, 1)), lhs_dilation=(2, 2),
        dimension_numbers=plain, preferred_element_type=F32,
    )
    grad_pre = (grad_act * silu_grad(pre_act)).astype(BF16)
    conv_part = lax.conv_general_dilated(
        block, grad_pre, (1, 1), "VALID", dimension_numbers=swapped, preferred_element_type=F32
    )
    conv_part = conv_part.transpose(1, 2, 3, 0).reshape(out_channels, conv_cols)
    w_back_conv = jnp.flip(w_conv, (2, 3)).transpose(1, 0, 2, 3)
    grad_block = lax.conv_general_dilated(
        grad_pre, w_back_conv, (1, 1), ((2, 2), (2, 2)), dimension_numbers=plain,
        preferred_element_type=F32,
    )

    pooled_out = jnp.moveaxis(pooled_rows.reshape(tiles, n_chan, out_share, rows // 2 * half), 1, 0)
    grad_out = jnp.moveaxis(
        grad_block.astype(BF16).reshape(tiles, n_chan, share, rows + 2, S + 2), 1, 0
    )
    down_dest = down_part.reshape(n_chan, out_share * down_cols)
    conv_dest = conv_part.reshape(n_chan, out_share, 9, in_channels).transpose(0, 2, 1, 3)
    w_part = jnp.concatenate([down_dest, conv_dest.reshape(n_chan, out_share * conv_cols)], axis=1)
    w_part = split_wide(w_part)
    pooled_in, w_back, grad_in = exchange([pooled_out, w_part, grad_out], "chan")
    pooled = jnp.moveaxis(pooled_in, 0, 2).reshape(tiles, out_share, half * half)
    w_sum = jnp.sum(join_wide(w_back), axis=0)

    g = grad_in.astype(F32)
    lead = jnp.concatenate([g[:1, :, :, :2, :], g[1:, :, :, :2, :] + g[:-1, :, :, rows:, :]], axis=0)
    body = jnp.concatenate([lead, g[:, :, :, 2:rows, :]], axis=3)
    grad_padded = jnp.concatenate(
        [jnp.moveaxis(body, 0, 2).reshape(tiles, share, S, S + 2), g[-1, :, :, rows:, :]], axis=2
    )

    rims = rim_strips(grad_padded)
    w_len = w_sum.shape[0]
    piece = -(-w_len // (n_space * 128)) * 128
    w_pieces = jnp.pad(w_sum, (0, piece * n_space - w_len)).reshape(n_space, piece)
    rims_all, w_got = exchange([to_all(rims.astype(BF16), n_space), split_wide(w_pieces)], "space")
    grad_scale = float(n_space * tiles * S * S) ** (-0.5)
    w_mine = jnp.sum(join_wide(w_got), axis=0) * grad_scale
    (w_all,) = exchange([to_all(w_mine, n_space)], "space")
    w_total = w_all.reshape(-1)[:w_len]

    returned = bordering(rims_all.reshape((n_space * tiles,) + rims.shape[1:]), partner, orientation)
    returned = returned.astype(F32)
    features_grad = add_edges(grad_padded[:, :, 1:-1, 1:-1], returned).astype(BF16)
    features_grad = features_grad.reshape(tiles, share, S * S)
    down_len = out_share * down_cols
    down_grad = w_total[:down_len].reshape(down_weight.shape)
    conv_grad = w_total[down_len:].reshape(9, out_share, in_channels).transpose(1, 0, 2)
    return (pooled, features_grad, conv_grad, down_grad)


def solution(mesh):
    placed = (
        P("space", "chan", None),
        P("chan", None, None),
        P("chan", None, None),
        P("space", "chan", None),
        P("space", None),
        P("space", None),
    )
    return jax.shard_map(
        shards,
        mesh=mesh,
        in_specs=placed,
        out_specs=(
            P("space", "chan", None),
            P("space", "chan", None),
            P("chan", None, None),
            P("chan", None, None),
        ),
        check_vma=False,
    )
```

```python
import jax
import jax.numpy as jnp
from jax import lax
from jax.sharding import PartitionSpec as P

S = 64
F32 = jnp.float32
BF16 = jnp.bfloat16


def edge_strips(values):
    return jnp.stack(
        [values[..., 0, :], values[..., :, -1], values[..., -1, :], values[..., :, 0]], axis=-3
    )


def rim_strips(padded):
    return jnp.stack(
        [padded[..., 0, 1:-1], padded[..., 1:-1, -1], padded[..., -1, 1:-1], padded[..., 1:-1, 0]],
        axis=-3,
    )


def bordering(strips, partner, orientation):
    flat = strips.reshape((-1,) + strips.shape[2:])
    picked = jnp.take(flat, partner.reshape(-1), axis=0)
    picked = picked.reshape(partner.shape + strips.shape[2:])
    return jnp.where((orientation == 1)[..., None, None], picked[..., ::-1], picked)


def pad_tile(values, halo_strips):
    tile_side = values.shape[-1]
    widths = [(0, 0)] * (values.ndim - 2) + [(1, 1), (1, 1)]
    padded = jnp.pad(values, widths)
    padded = padded.at[..., 0, 1 : tile_side + 1].set(halo_strips[..., 0, :, :])
    padded = padded.at[..., 1 : tile_side + 1, tile_side + 1].set(halo_strips[..., 1, :, :])
    padded = padded.at[..., tile_side + 1, 1 : tile_side + 1].set(halo_strips[..., 2, :, :])
    return padded.at[..., 1 : tile_side + 1, 0].set(halo_strips[..., 3, :, :])


def pad_cat(values, halo):
    zero = jnp.zeros(values.shape[:2] + (1, 1), values.dtype)
    top = jnp.concatenate([zero, halo[:, 0, :, None, :], zero], axis=3)
    bottom = jnp.concatenate([zero, halo[:, 2, :, None, :], zero], axis=3)
    middle = jnp.concatenate([halo[:, 3, :, :, None], values, halo[:, 1, :, :, None]], axis=3)
    return jnp.concatenate([top, middle, bottom], axis=2)


def add_edges(interior, returned):
    n = interior.shape[-1]
    none = ((0, 0), (0, 0))
    rows = jnp.pad(returned[:, 0, :, None, :], none + ((0, n - 1), (0, 0))) + jnp.pad(
        returned[:, 2, :, None, :], none + ((n - 1, 0), (0, 0))
    )
    cols = jnp.pad(returned[:, 3, :, :, None], none + ((0, 0), (0, n - 1))) + jnp.pad(
        returned[:, 1, :, :, None], none + ((0, 0), (n - 1, 0))
    )
    return interior + (rows + cols)


def unfold(padded, height, width):
    taps = [
        padded[..., row_shift : row_shift + height, col_shift : col_shift + width]
        for row_shift in range(3)
        for col_shift in range(3)
    ]
    return jnp.stack(taps, axis=-4)


def fold_taps(taps):
    total = None
    for row_shift in range(3):
        for col_shift in range(3):
            piece = taps[..., 3 * row_shift + col_shift, :, :, :]
            widths = [(0, 0)] * (piece.ndim - 2) + [
                (row_shift, 2 - row_shift),
                (col_shift, 2 - col_shift),
            ]
            placed = jnp.pad(piece, widths)
            total = placed if total is None else total + placed
    return total


def silu_grad(values):
    gate = jax.nn.sigmoid(values)
    return gate * (1.0 + values * (1.0 - gate))


def exchange(parts, axis):
    count = parts[0].shape[0]
    tile = 4096 // parts[0].dtype.itemsize
    flat = []
    for i, p in enumerate(parts):
        size = p[0].size
        step = 128 if i == len(parts) - 1 else tile
        padded = jnp.pad(p.reshape(count, size), ((0, 0), (0, -size % step)))
        flat.append(padded.reshape(count, -1, 128))
    got = lax.all_to_all(jnp.concatenate(flat, axis=1), axis, 0, 0, tiled=True)
    out, start = [], 0
    for p, f in zip(parts, flat):
        piece = got[:, start : start + f.shape[1]].reshape(count, -1)
        out.append(piece[:, : p[0].size].reshape(p.shape))
        start += f.shape[1]
    return out


def to_all(value, count):
    return jnp.broadcast_to(value[None], (count,) + value.shape)


def split_wide(value):
    high = lax.reduce_precision(value, exponent_bits=8, mantissa_bits=7)
    return jnp.concatenate([high, value - high], axis=-1).astype(BF16)


def join_wide(value):
    half = value.shape[-1] // 2
    wide = value.astype(F32)
    return wide[..., :half] + wide[..., half:]


def shards(features, conv_weight, down_weight, cotangent, partner, orientation):
    tiles, share, _ = features.shape
    n_chan = lax.axis_size("chan")
    n_space = lax.axis_size("space")
    in_channels = share * n_chan
    out_share = conv_weight.shape[0]
    out_channels = out_share * n_chan
    rows = S // n_chan
    half = S // 2
    conv_cols = conv_weight.shape[1] * conv_weight.shape[2]
    down_cols = down_weight.shape[1] * down_weight.shape[2]

    weights = jnp.concatenate(
        [conv_weight.reshape(out_share, conv_cols), down_weight.reshape(out_share, down_cols)], axis=1
    )

    images = features.reshape(tiles, share, S, S)
    strips = edge_strips(images)
    (strips_all,) = exchange([to_all(strips, n_space)], "space")
    halo = bordering(strips_all.reshape((n_space * tiles,) + strips.shape[1:]), partner, orientation)
    padded = pad_cat(images, halo)

    head = padded[:, :, : S, :].reshape(tiles, share, n_chan, rows, S + 2)
    tail = jnp.pad(padded[:, :, rows:, :], ((0, 0), (0, 0), (0, rows - 2), (0, 0)))
    tail = tail.reshape(tiles, share, n_chan, rows, S + 2)[:, :, :, :2, :]
    bands = jnp.moveaxis(jnp.concatenate([head, tail], axis=3), 2, 0)
    cot_bands = jnp.moveaxis(cotangent.reshape(tiles, out_share, n_chan, rows // 2 * half), 2, 0)
    cot_in, w_in, band_in = exchange([cot_bands, to_all(weights, n_chan), bands], "chan")
    block = jnp.moveaxis(band_in, 0, 1).reshape(tiles, in_channels, rows + 2, S + 2)
    grad_band = jnp.moveaxis(cot_in, 0, 1).reshape(tiles, out_channels, rows // 2, half)
    w_full = w_in.reshape(out_channels, conv_cols + down_cols)
    conv_full = w_full[:, :conv_cols].reshape(out_channels, 9, in_channels)
    down_full = w_full[:, conv_cols:].reshape(out_channels, 4, out_channels)

    plain = ("NCHW", "OIHW", "NCHW")
    swapped = ("CNHW", "IOHW", "NCHW")
    w_conv = conv_full.reshape(out_channels, 3, 3, in_channels).transpose(0, 3, 1, 2)
    w_down = down_full.reshape(out_channels, 2, 2, out_channels).transpose(0, 3, 1, 2)
    pre_act = lax.conv_general_dilated(
        block, w_conv, (1, 1), "VALID", dimension_numbers=plain, preferred_element_type=F32
    )
    activated = jax.nn.silu(pre_act).astype(BF16)
    pooled_rows = lax.conv_general_dilated(
        activated, w_down, (2, 2), "VALID", dimension_numbers=plain, preferred_element_type=F32
    ).astype(BF16)
    down_part = lax.conv_general_dilated(
        activated, grad_band, (1, 1), "VALID", rhs_dilation=(2, 2),
        dimension_numbers=swapped, preferred_element_type=F32,
    )
    down_part = down_part.transpose(1, 2, 3, 0).reshape(out_channels, down_cols)
    taps = down_full.reshape(out_channels, 2, 2, out_channels)
    grad_act = jnp.einsum("opqc,touv->tcupvq", taps, grad_band, preferred_element_type=F32)
    grad_act = grad_act.reshape(tiles, out_channels, rows, S)
    grad_pre = (grad_act * silu_grad(pre_act)).astype(BF16)
    conv_part = lax.conv_general_dilated(
        block, grad_pre, (1, 1), "VALID", dimension_numbers=swapped, preferred_element_type=F32
    )
    conv_part = conv_part.transpose(1, 2, 3, 0).reshape(out_channels, conv_cols)
    w_back_conv = jnp.flip(w_conv, (2, 3)).transpose(1, 0, 2, 3)
    grad_block = lax.conv_general_dilated(
        grad_pre, w_back_conv, (1, 1), ((2, 2), (2, 2)), dimension_numbers=plain,
        preferred_element_type=F32,
    )

    pooled_out = jnp.moveaxis(pooled_rows.reshape(tiles, n_chan, out_share, rows // 2 * half), 1, 0)
    grad_out = jnp.moveaxis(
        grad_block.astype(BF16).reshape(tiles, n_chan, share, rows + 2, S + 2), 1, 0
    )
    down_dest = down_part.reshape(n_chan, out_share * down_cols)
    conv_dest = conv_part.reshape(n_chan, out_share, 9, in_channels).transpose(0, 2, 1, 3)
    w_part = jnp.concatenate([down_dest, conv_dest.reshape(n_chan, out_share * conv_cols)], axis=1)
    w_part = split_wide(w_part)
    pooled_in, w_back, grad_in = exchange([pooled_out, w_part, grad_out], "chan")
    pooled = jnp.moveaxis(pooled_in, 0, 2).reshape(tiles, out_share, half * half)
    w_sum = jnp.sum(join_wide(w_back), axis=0)

    g = grad_in.astype(F32)
    lead = jnp.concatenate([g[:1, :, :, :2, :], g[1:, :, :, :2, :] + g[:-1, :, :, rows:, :]], axis=0)
    body = jnp.concatenate([lead, g[:, :, :, 2:rows, :]], axis=3)
    grad_padded = jnp.concatenate(
        [jnp.moveaxis(body, 0, 2).reshape(tiles, share, S, S + 2), g[-1, :, :, rows:, :]], axis=2
    )

    rims = rim_strips(grad_padded)
    w_len = w_sum.shape[0]
    piece = -(-w_len // (n_space * 128)) * 128
    w_pieces = jnp.pad(w_sum, (0, piece * n_space - w_len)).reshape(n_space, piece)
    rims_all, w_got = exchange([to_all(rims.astype(BF16), n_space), split_wide(w_pieces)], "space")
    grad_scale = float(n_space * tiles * S * S) ** (-0.5)
    w_mine = jnp.sum(join_wide(w_got), axis=0) * grad_scale
    (w_all,) = exchange([to_all(w_mine, n_space)], "space")
    w_total = w_all.reshape(-1)[:w_len]

    returned = bordering(rims_all.reshape((n_space * tiles,) + rims.shape[1:]), partner, orientation)
    returned = returned.astype(F32)
    features_grad = add_edges(grad_padded[:, :, 1:-1, 1:-1], returned).astype(BF16)
    features_grad = features_grad.reshape(tiles, share, S * S)
    down_len = out_share * down_cols
    down_grad = w_total[:down_len].reshape(down_weight.shape)
    conv_grad = w_total[down_len:].reshape(9, out_share, in_channels).transpose(1, 0, 2)
    return (pooled, features_grad, conv_grad, down_grad)


def solution(mesh):
    placed = (
        P("space", "chan", None),
        P("chan", None, None),
        P("chan", None, None),
        P("space", "chan", None),
        P("space", None),
        P("space", None),
    )
    return jax.shard_map(
        shards,
        mesh=mesh,
        in_specs=placed,
        out_specs=(
            P("space", "chan", None),
            P("space", "chan", None),
            P("chan", None, None),
            P("chan", None, None),
        ),
        check_vma=False,
    )
```

```python
import jax
import jax.numpy as jnp
from jax import lax
from jax.sharding import PartitionSpec as P

S = 64
F32 = jnp.float32
BF16 = jnp.bfloat16


def edge_strips(values):
    return jnp.stack(
        [values[..., 0, :], values[..., :, -1], values[..., -1, :], values[..., :, 0]], axis=-3
    )


def rim_strips(padded):
    return jnp.stack(
        [padded[..., 0, 1:-1], padded[..., 1:-1, -1], padded[..., -1, 1:-1], padded[..., 1:-1, 0]],
        axis=-3,
    )


def bordering(strips, partner, orientation):
    flat = strips.reshape((-1,) + strips.shape[2:])
    picked = jnp.take(flat, partner.reshape(-1), axis=0)
    picked = picked.reshape(partner.shape + strips.shape[2:])
    return jnp.where((orientation == 1)[..., None, None], picked[..., ::-1], picked)


def pad_tile(values, halo_strips):
    tile_side = values.shape[-1]
    widths = [(0, 0)] * (values.ndim - 2) + [(1, 1), (1, 1)]
    padded = jnp.pad(values, widths)
    padded = padded.at[..., 0, 1 : tile_side + 1].set(halo_strips[..., 0, :, :])
    padded = padded.at[..., 1 : tile_side + 1, tile_side + 1].set(halo_strips[..., 1, :, :])
    padded = padded.at[..., tile_side + 1, 1 : tile_side + 1].set(halo_strips[..., 2, :, :])
    return padded.at[..., 1 : tile_side + 1, 0].set(halo_strips[..., 3, :, :])


def pad_cat(values, halo):
    zero = jnp.zeros(values.shape[:2] + (1, 1), values.dtype)
    top = jnp.concatenate([zero, halo[:, 0, :, None, :], zero], axis=3)
    bottom = jnp.concatenate([zero, halo[:, 2, :, None, :], zero], axis=3)
    middle = jnp.concatenate([halo[:, 3, :, :, None], values, halo[:, 1, :, :, None]], axis=3)
    return jnp.concatenate([top, middle, bottom], axis=2)


def add_edges(interior, returned):
    n = interior.shape[-1]
    none = ((0, 0), (0, 0))
    rows = jnp.pad(returned[:, 0, :, None, :], none + ((0, n - 1), (0, 0))) + jnp.pad(
        returned[:, 2, :, None, :], none + ((n - 1, 0), (0, 0))
    )
    cols = jnp.pad(returned[:, 3, :, :, None], none + ((0, 0), (0, n - 1))) + jnp.pad(
        returned[:, 1, :, :, None], none + ((0, 0), (n - 1, 0))
    )
    return interior + (rows + cols)


def unfold(padded, height, width):
    taps = [
        padded[..., row_shift : row_shift + height, col_shift : col_shift + width]
        for row_shift in range(3)
        for col_shift in range(3)
    ]
    return jnp.stack(taps, axis=-4)


def fold_taps(taps):
    total = None
    for row_shift in range(3):
        for col_shift in range(3):
            piece = taps[..., 3 * row_shift + col_shift, :, :, :]
            widths = [(0, 0)] * (piece.ndim - 2) + [
                (row_shift, 2 - row_shift),
                (col_shift, 2 - col_shift),
            ]
            placed = jnp.pad(piece, widths)
            total = placed if total is None else total + placed
    return total


def silu_grad(values):
    gate = jax.nn.sigmoid(values)
    return gate * (1.0 + values * (1.0 - gate))


def exchange(parts, axis):
    count = parts[0].shape[0]
    tile = 4096 // parts[0].dtype.itemsize
    flat = []
    for i, p in enumerate(parts):
        size = p[0].size
        step = 128 if i == len(parts) - 1 else tile
        padded = jnp.pad(p.reshape(count, size), ((0, 0), (0, -size % step)))
        flat.append(padded.reshape(count, -1, 128))
    got = lax.all_to_all(jnp.concatenate(flat, axis=1), axis, 0, 0, tiled=True)
    out, start = [], 0
    for p, f in zip(parts, flat):
        piece = got[:, start : start + f.shape[1]].reshape(count, -1)
        out.append(piece[:, : p[0].size].reshape(p.shape))
        start += f.shape[1]
    return out


def to_all(value, count):
    return jnp.broadcast_to(value[None], (count,) + value.shape)


def split_wide(value):
    high = lax.reduce_precision(value, exponent_bits=8, mantissa_bits=7)
    return jnp.concatenate([high, value - high], axis=-1).astype(BF16)


def join_wide(value):
    half = value.shape[-1] // 2
    wide = value.astype(F32)
    return wide[..., :half] + wide[..., half:]


def shards(features, conv_weight, down_weight, cotangent, partner, orientation):
    tiles, share, _ = features.shape
    n_chan = lax.axis_size("chan")
    n_space = lax.axis_size("space")
    in_channels = share * n_chan
    out_share = conv_weight.shape[0]
    out_channels = out_share * n_chan
    rows = S // n_chan
    half = S // 2
    conv_cols = conv_weight.shape[1] * conv_weight.shape[2]
    down_cols = down_weight.shape[1] * down_weight.shape[2]

    weights = jnp.concatenate(
        [conv_weight.reshape(out_share, conv_cols), down_weight.reshape(out_share, down_cols)], axis=1
    )

    images = features.reshape(tiles, share, S, S)
    strips = edge_strips(images)
    (strips_all,) = exchange([to_all(strips, n_space)], "space")
    halo = bordering(strips_all.reshape((n_space * tiles,) + strips.shape[1:]), partner, orientation)
    padded = pad_cat(images, halo)

    head = padded[:, :, : S, :].reshape(tiles, share, n_chan, rows, S + 2)
    tail = jnp.pad(padded[:, :, rows:, :], ((0, 0), (0, 0), (0, rows - 2), (0, 0)))
    tail = tail.reshape(tiles, share, n_chan, rows, S + 2)[:, :, :, :2, :]
    bands = jnp.moveaxis(jnp.concatenate([head, tail], axis=3), 2, 0)
    cot_bands = jnp.moveaxis(cotangent.reshape(tiles, out_share, n_chan, rows // 2 * half), 2, 0)
    cot_in, w_in, band_in = exchange([cot_bands, to_all(weights, n_chan), bands], "chan")
    block = jnp.moveaxis(band_in, 0, 1).reshape(tiles, in_channels, rows + 2, S + 2)
    grad_band = jnp.moveaxis(cot_in, 0, 1).reshape(tiles, out_channels, rows // 2, half)
    w_full = w_in.reshape(out_channels, conv_cols + down_cols)
    conv_full = w_full[:, :conv_cols].reshape(out_channels, 9, in_channels)
    down_full = w_full[:, conv_cols:].reshape(out_channels, 4, out_channels)

    plain = ("NCHW", "OIHW", "NCHW")
    swapped = ("CNHW", "IOHW", "NCHW")
    w_conv = conv_full.reshape(out_channels, 3, 3, in_channels).transpose(0, 3, 1, 2)
    w_down = down_full.reshape(out_channels, 2, 2, out_channels).transpose(0, 3, 1, 2)
    pre_act = lax.conv_general_dilated(
        block, w_conv, (1, 1), "VALID", dimension_numbers=plain, preferred_element_type=F32
    )
    activated = jax.nn.silu(pre_act).astype(BF16)
    pooled_rows = lax.conv_general_dilated(
        activated, w_down, (2, 2), "VALID", dimension_numbers=plain, preferred_element_type=F32
    ).astype(BF16)
    quads = activated.reshape(tiles, out_channels, rows // 2, 2, half, 2)
    down_part = jnp.einsum("touv,tcupvq->opqc", grad_band, quads, preferred_element_type=F32)
    down_part = down_part.reshape(out_channels, down_cols)
    w_up = jnp.flip(w_down, (2, 3)).transpose(1, 0, 2, 3)
    grad_act = lax.conv_general_dilated(
        grad_band, w_up, (1, 1), ((1, 1), (1, 1)), lhs_dilation=(2, 2),
        dimension_numbers=plain, preferred_element_type=F32,
    )
    grad_pre = (grad_act * silu_grad(pre_act)).astype(BF16)
    conv_part = lax.conv_general_dilated(
        block, grad_pre, (1, 1), "VALID", dimension_numbers=swapped, preferred_element_type=F32
    )
    conv_part = conv_part.transpose(1, 2, 3, 0).reshape(out_channels, conv_cols)
    w_back_conv = jnp.flip(w_conv, (2, 3)).transpose(1, 0, 2, 3)
    grad_block = lax.conv_general_dilated(
        grad_pre, w_back_conv, (1, 1), ((2, 2), (2, 2)), dimension_numbers=plain,
        preferred_element_type=F32,
    )

    pooled_out = jnp.moveaxis(pooled_rows.reshape(tiles, n_chan, out_share, rows // 2 * half), 1, 0)
    grad_out = jnp.moveaxis(
        grad_block.astype(BF16).reshape(tiles, n_chan, share, rows + 2, S + 2), 1, 0
    )
    down_dest = down_part.reshape(n_chan, out_share * down_cols)
    conv_dest = conv_part.reshape(n_chan, out_share, 9, in_channels).transpose(0, 2, 1, 3)
    w_part = jnp.concatenate([down_dest, conv_dest.reshape(n_chan, out_share * conv_cols)], axis=1)
    w_part = split_wide(w_part)
    pooled_in, w_back, grad_in = exchange([pooled_out, w_part, grad_out], "chan")
    pooled = jnp.moveaxis(pooled_in, 0, 2).reshape(tiles, out_share, half * half)
    w_sum = jnp.sum(join_wide(w_back), axis=0)

    g = grad_in.astype(F32)
    lead = jnp.concatenate([g[:1, :, :, :2, :], g[1:, :, :, :2, :] + g[:-1, :, :, rows:, :]], axis=0)
    body = jnp.concatenate([lead, g[:, :, :, 2:rows, :]], axis=3)
    grad_padded = jnp.concatenate(
        [jnp.moveaxis(body, 0, 2).reshape(tiles, share, S, S + 2), g[-1, :, :, rows:, :]], axis=2
    )

    rims = rim_strips(grad_padded)
    w_len = w_sum.shape[0]
    piece = -(-w_len // (n_space * 128)) * 128
    w_pieces = jnp.pad(w_sum, (0, piece * n_space - w_len)).reshape(n_space, piece)
    rims_all, w_got = exchange([to_all(rims.astype(BF16), n_space), split_wide(w_pieces)], "space")
    grad_scale = float(n_space * tiles * S * S) ** (-0.5)
    w_mine = jnp.sum(join_wide(w_got), axis=0) * grad_scale
    (w_all,) = exchange([to_all(w_mine, n_space)], "space")
    w_total = w_all.reshape(-1)[:w_len]

    returned = bordering(rims_all.reshape((n_space * tiles,) + rims.shape[1:]), partner, orientation)
    returned = returned.astype(F32)
    features_grad = add_edges(grad_padded[:, :, 1:-1, 1:-1], returned).astype(BF16)
    features_grad = features_grad.reshape(tiles, share, S * S)
    down_len = out_share * down_cols
    down_grad = w_total[:down_len].reshape(down_weight.shape)
    conv_grad = w_total[down_len:].reshape(9, out_share, in_channels).transpose(1, 0, 2)
    return (pooled, features_grad, conv_grad, down_grad)


def solution(mesh):
    placed = (
        P("space", "chan", None),
        P("chan", None, None),
        P("chan", None, None),
        P("space", "chan", None),
        P("space", None),
        P("space", None),
    )
    return jax.shard_map(
        shards,
        mesh=mesh,
        in_specs=placed,
        out_specs=(
            P("space", "chan", None),
            P("space", "chan", None),
            P("chan", None, None),
            P("chan", None, None),
        ),
        check_vma=False,
    )
```
